768 devices in a mesh: blk: 192 (over z, y, core), sub: 4 (over x).
Axes of the slice: x: 4, y: 8, z: 12, core: 2. Of those that a mesh axis runs over, the one named last changes fastest.
Arguments:
- adj_source: float32 [6, 6144, 2048], P(None, 'blk', 'sub'), may hold values from -6 to 6
- jac_diag: float32 [6, 6, 6144, 2048], P(None, None, 'blk', 'sub'), may hold values from -0.6 to 0.6
- face_weights: float32 [8, 6144, 2048], P(None, 'blk', 'sub'), may hold values from 0.02 to 0.12
- flux_jac: float32 [8, 6, 6], replicated, may hold values from -1.25 to 1.25
- face_link: int32 [192], replicated, may hold values 0 or 1
- node_grad: bfloat16 [3, 6, 6144, 2048], P(None, None, 'blk', 'sub'), may hold values from -2.5 to 2.5
- stiffness: float32 [6144, 2048], P(('blk', 'sub')), may hold values from 0.5 to 5
Outputs:
- adjoint: float32 [6, 6144, 2048], P(None, 'blk', 'sub')
- warp_adjoint: float32 [3, 6144, 2048], P(None, ('blk', 'sub'))
The draws below stay inside these ranges and needn't reach their ends.
Inputs may be any that keep to these rules, and one draw needn't show every extreme that they name: `face_link`: 1 where a block's upper face meets the next block along the first grid direction, the last block's meeting the first.
All inputs are finite; a program needn't handle non-finite values.
Results may differ from the reference program's by a relative error of at most 0.0005.
Values sent between devices are 32-bit elements; how exact they have to be, the bound alone decides.
No kernel may reach another device: no remote copies, remote signals or barrier semaphores. Data moves between devices by JAX's collectives and lax.ppermute only.
A program may use at most 64 MiB of HBM per device.

```python
import math
import jax
import jax.numpy as jnp
from jax import lax

NF = 6
NCOMP = 3
NDIR = 8
ITERS = 4
SWEEPS = 6
CI = 32
NI = 6144
NJ = 2048
N_BLK = 192


def set_ends(values, own_key, low, largest):
    index_at = [jax.random.randint(jax.random.fold_in(own_key, axis), (), 0, length) for axis, length in enumerate(values.shape)]
    main_axis = values.shape.index(max(values.shape))
    beside = index_at[:main_axis] + [(index_at[main_axis] + 1) % values.shape[main_axis]] + index_at[main_axis + 1:]
    return values.at[tuple(index_at)].set(low).at[tuple(beside)].set(largest)


def level_of(stream_key, extent, shards, least, high):
    factor_of = 1.0
    for position, shards_of in shards:
        draws = jax.random.uniform(jax.random.fold_in(jax.random.fold_in(stream_key, 6), position), (shards_of,), jnp.float32, least / len(shards), high / len(shards))
        factor_of = factor_of * jnp.repeat(jnp.exp(draws), extent[position] // shards_of).reshape((-1,) + (1,) * (len(extent) - 1 - position))
    return factor_of


def noise(key, dims, deviation, limit, pieces=(), kind=jnp.bfloat16):
    drawn = jax.random.normal(key, dims, jnp.float32) * deviation
    if len(pieces) > 0:
        drawn = level_of(key, dims, pieces, -0.22, 0.18) * drawn
    return jnp.clip(drawn, min=-limit, max=limit).astype(kind)


def setup_inputs(seed: int = 0) -> dict:
    key_of = jax.random.split(jax.random.key(seed), 8)
    adj_source = noise(key_of[0], (NF, NI, NJ), 1.0, 6.0, ((1, 192), (2, 4)), jnp.float32)
    jac_diag = noise(key_of[1], (NF, NF, NI, NJ), 0.12, 0.6, ((2, 192), (3, 4)), jnp.float32)
    face_weights = jnp.clip(jnp.exp(math.log(0.12) - 1.7917595 * jax.random.uniform(key_of[2], (NDIR, NI, NJ), jnp.float32) ** level_of(key_of[2], (NDIR, NI, NJ), ((1, 192), (2, 4)), -0.2, 0.2)), 0.02, 0.12)
    flux_jac = noise(key_of[3], (NDIR, NF, NF), (4 * NF) ** -0.5, 1.25, (), jnp.float32)
    face_link = set_ends((jax.random.randint(key_of[4], (N_BLK,), 0, 4) < 3).astype(jnp.int32), jax.random.fold_in(key_of[4], 1), 0, 1)
    node_grad = noise(key_of[5], (NCOMP, NF, NI, NJ), NF ** -0.5, 2.5, ((2, 192), (3, 4)))
    stiffness = jnp.clip(jnp.exp(math.log(5.0) - 2.3025851 * jax.random.uniform(key_of[6], (NI, NJ), jnp.float32) ** level_of(key_of[6], (NI, NJ), ((0, 768),), -0.2, 0.2)), 0.5, 5.0)
    return {"adj_source": adj_source, "jac_diag": jac_diag, "face_weights": face_weights, "flux_jac": flux_jac, "face_link": face_link, "node_grad": node_grad, "stiffness": stiffness}


relax_factor = 0.8
couple_factor = 2.0 / 9.0
offsets_table = ((1, 0), (-1, 0), (2, 0), (-2, 0), (0, 1), (0, -1), (0, 2), (0, -2))

def neighbour(field, row_step, col_step, face_link):
    total_rows = field.shape[1]
    moved = jnp.roll(field, (-row_step, -col_step), axis=(1, 2))
    if row_step == 0:
        return moved
    row_ids = jnp.arange(total_rows, dtype=jnp.int32)
    block_here = row_ids // CI
    block_there = (row_ids + row_step) % total_rows // CI
    crossing = block_here != block_there
    if row_step > 0:
        face_index = block_here
    else:
        face_index = (block_here - 1 + N_BLK) % N_BLK
    link_value = face_link[face_index].astype(jnp.float32)
    factor = jnp.where(crossing, link_value, jnp.ones_like(link_value))
    return moved * factor[None, :, None]

def transposed_residual(adjoint, jac_diag, face_weights, flux_jac, face_link):
    result = adjoint + jnp.einsum('fgij,gij->fij', jac_diag, adjoint, precision=lax.Precision.HIGHEST)
    for direction in range(8):
        row_step, col_step = offsets_table[direction]
        shifted = neighbour(adjoint, row_step, col_step, face_link)
        mixed = jnp.einsum('fg,gij->fij', flux_jac[direction], shifted, precision=lax.Precision.HIGHEST)
        result = result - face_weights[direction][None] * mixed
    return result

def reference(adj_source, jac_diag, face_weights, flux_jac, face_link, node_grad, stiffness):
    adjoint = adj_source
    for iteration in range(ITERS):
        image = transposed_residual(adjoint, jac_diag, face_weights, flux_jac, face_link)
        adjoint = adjoint + relax_factor * (adj_source - image)
    sensitivity = jnp.einsum('cfij,fij->cij', node_grad.astype(jnp.float32), adjoint, precision=lax.Precision.HIGHEST)
    root_stiff = jnp.sqrt(stiffness)
    base_term = sensitivity / stiffness[None]
    scale_term = couple_factor / root_stiff
    warp_adjoint = jnp.zeros_like(sensitivity)
    for sweep_index in range(SWEEPS):
        spread = root_stiff[None] * warp_adjoint
        padded = jnp.pad(spread, ((0, 0), (1, 1), (0, 0)))
        beside_all = padded[:, :-2] + padded[:, 2:] + jnp.roll(spread, 1, 2) + jnp.roll(spread, -1, 2)
        warp_adjoint = base_term + scale_term[None] * beside_all
    return (adjoint, warp_adjoint)
```

```python
import numpy as np
import jax
import jax.numpy as jnp
from jax import lax
from jax.sharding import PartitionSpec as P

ITERS = 4
SWEEPS = 6


relax_factor = 0.8
couple_factor = 2.0 / 9.0
offsets_table = ((1, 0), (-1, 0), (2, 0), (-2, 0), (0, 1), (0, -1), (0, 2), (0, -2))
REACH = 2


def ring_pairs(count, periodic):
    forward = [(i, i + 1) for i in range(count - 1)]
    if periodic:
        forward.append((count - 1, 0))
    backward = [(target, source) for source, target in forward]
    return forward, backward


def pack(parts):
    return jnp.concatenate([part.reshape(-1) for part in parts])


def unpack(flat, shapes):
    out = []
    start = 0
    for shape in shapes:
        size = int(np.prod(shape))
        out.append(flat[start : start + size].reshape(shape))
        start += size
    return out


def exchange(arrays, widths, axis, dim, periodic):
    count = lax.axis_size(axis)
    forward, backward = ring_pairs(count, periodic)
    lows = [lax.slice_in_dim(a, a.shape[dim] - w, None, axis=dim) for a, w in zip(arrays, widths)]
    highs = [lax.slice_in_dim(a, 0, w, axis=dim) for a, w in zip(arrays, widths)]
    shapes = [x.shape for x in lows]
    got_low = unpack(lax.ppermute(pack(lows), axis, forward), shapes)
    got_high = unpack(lax.ppermute(pack(highs), axis, backward), shapes)
    return [
        jnp.concatenate([lo, a, hi], axis=dim) for lo, a, hi in zip(got_low, arrays, got_high)
    ]


def local(adj_source, jac_diag, face_weights, flux_jac, face_link, node_grad, stiffness):
    block_index = lax.axis_index("blk")
    block_count = lax.axis_size("blk")
    link_above = face_link[block_index].astype(jnp.float32)
    link_below = face_link[(block_index + block_count - 1) % block_count].astype(jnp.float32)
    nf = adj_source.shape[0]
    rows_here = adj_source.shape[1]
    cols_here = adj_source.shape[2]
    deep = REACH * ITERS
    deep_coef = REACH * (ITERS - 1)

    src_x, jd_x, fw_x = exchange(
        [adj_source, jac_diag.reshape((nf * nf,) + jac_diag.shape[2:]), face_weights],
        [deep, deep_coef, deep_coef],
        "blk",
        1,
        True,
    )
    src_x, jd_x, fw_x = exchange([src_x, jd_x, fw_x], [deep, deep_coef, deep_coef], "sub", 2, True)
    jd_x = jd_x.reshape((nf, nf) + jd_x.shape[1:])

    flux_all = flux_jac.reshape((-1, nf))

    def row_factor(margin, row_step):
        rows = np.arange(-margin, rows_here + margin)
        here = np.floor_divide(rows, rows_here)
        there = np.floor_divide(rows + row_step, rows_here)
        face = np.minimum(here, there)
        cross_below = jnp.asarray((here != there) & (face < 0))
        cross_above = jnp.asarray((here != there) & (face >= 0))
        unit = jnp.ones((rows.shape[0],), jnp.float32)
        return jnp.where(cross_above, link_above * unit, jnp.where(cross_below, link_below * unit, unit))

    adjoint = src_x
    for iteration in range(ITERS):
        margin_in = deep - REACH * iteration
        margin = margin_in - REACH
        out_rows = rows_here + 2 * margin
        out_cols = cols_here + 2 * margin
        c0 = deep_coef - margin
        s0 = deep - margin
        centre = adjoint[:, REACH : REACH + out_rows, REACH : REACH + out_cols]
        jd = jd_x[:, :, c0 : c0 + out_rows, c0 : c0 + out_cols]
        fw = fw_x[:, c0 : c0 + out_rows, c0 : c0 + out_cols]
        src = src_x[:, s0 : s0 + out_rows, s0 : s0 + out_cols]
        result = centre + jnp.einsum("fgij,gij->fij", jd, centre, precision=lax.Precision.HIGHEST)
        mixed_all = jnp.einsum(
            "eg,gij->eij", flux_all, adjoint, precision=lax.Precision.HIGHEST
        ).reshape((len(offsets_table), nf) + adjoint.shape[1:])
        for direction in range(len(offsets_table)):
            row_step, col_step = offsets_table[direction]
            mixed = mixed_all[
                direction,
                :,
                REACH + row_step : REACH + row_step + out_rows,
                REACH + col_step : REACH + col_step + out_cols,
            ]
            if row_step != 0:
                mixed = mixed * row_factor(margin, row_step)[None, :, None]
            result = result - fw[direction][None] * mixed
        adjoint = centre + relax_factor * (src - result)

    sensitivity = jnp.einsum(
        "cfij,fij->cij", node_grad.astype(jnp.float32), adjoint, precision=lax.Precision.HIGHEST
    )
    moved = lax.all_to_all(sensitivity, "sub", split_axis=1, concat_axis=2, tiled=True)

    part_axis = ("blk", "sub")
    part_index = block_index * lax.axis_size("sub") + lax.axis_index("sub")
    part_count = block_count * lax.axis_size("sub")
    warp_rows = moved.shape[1]
    halo = SWEEPS - 1
    both = jnp.concatenate([moved, stiffness[None]], axis=0)
    (both_x,) = exchange([both], [halo], part_axis, 1, False)
    global_rows = part_index * warp_rows + jnp.arange(-halo, warp_rows + halo, dtype=jnp.int32)
    valid = (global_rows >= 0) & (global_rows < part_count * warp_rows)
    sens_x = both_x[:-1]
    stiff_x = jnp.where(valid[:, None], both_x[-1], 1.0)
    root_stiff = jnp.sqrt(stiff_x)
    base_term = sens_x / stiff_x[None]
    scale_term = couple_factor / root_stiff
    warp_adjoint = base_term
    for sweep_index in range(1, SWEEPS):
        margin_in = halo - (sweep_index - 1)
        margin = margin_in - 1
        lo = halo - margin_in
        hi = lo + warp_rows + 2 * margin_in
        spread = jnp.where(valid[lo:hi, None][None], root_stiff[lo:hi][None] * warp_adjoint, 0.0)
        inner = spread[:, 1:-1]
        beside_all = (
            spread[:, :-2] + spread[:, 2:] + jnp.roll(inner, 1, 2) + jnp.roll(inner, -1, 2)
        )
        olo = halo - margin
        ohi = olo + warp_rows + 2 * margin
        warp_adjoint = base_term[:, olo:ohi] + scale_term[olo:ohi][None] * beside_all
    return (adjoint, warp_adjoint)


def solution(mesh):
    placed = (
        P(None, "blk", "sub"),
        P(None, None, "blk", "sub"),
        P(None, "blk", "sub"),
        P(),
        P(),
        P(None, None, "blk", "sub"),
        P(("blk", "sub"), None),
    )
    return jax.shard_map(
        local,
        mesh=mesh,
        in_specs=placed,
        out_specs=(P(None, "blk", "sub"), P(None, ("blk", "sub"), None)),
        check_vma=False,
    )
```

```python
import numpy as np
import jax
import jax.numpy as jnp
from jax import lax
from jax.sharding import PartitionSpec as P

ITERS = 4
SWEEPS = 6


relax_factor = 0.8
couple_factor = 2.0 / 9.0
offsets_table = ((1, 0), (-1, 0), (2, 0), (-2, 0), (0, 1), (0, -1), (0, 2), (0, -2))
REACH = 2
LANES = 128


def ring_pairs(count, periodic):
    forward = [(i, i + 1) for i in range(count - 1)]
    if periodic:
        forward.append((count - 1, 0))
    backward = [(target, source) for source, target in forward]
    return forward, backward


def local(adj_source, jac_diag, face_weights, flux_jac, face_link, node_grad, stiffness):
    block_index = lax.axis_index("blk")
    block_count = lax.axis_size("blk")
    link_above = face_link[block_index].astype(jnp.float32)
    link_below = face_link[(block_index + block_count - 1) % block_count].astype(jnp.float32)
    nf = adj_source.shape[0]
    rows_here = adj_source.shape[1]
    cols_here = adj_source.shape[2]
    deep = REACH * ITERS
    width = -(-(cols_here + 2 * deep) // LANES) * LANES

    stack = jnp.concatenate(
        [adj_source, jac_diag.reshape((nf * nf,) + jac_diag.shape[2:]), face_weights], axis=0
    )
    forward, backward = ring_pairs(block_count, True)
    from_below = lax.ppermute(stack[:, rows_here - deep :], "blk", forward)
    from_above = lax.ppermute(stack[:, :deep], "blk", backward)
    tall = jnp.concatenate([stack, from_above, from_below], axis=1)
    sub_count = lax.axis_size("sub")
    forward, backward = ring_pairs(sub_count, True)
    edge_shape = tall[:, :, :deep].shape
    from_left = lax.ppermute(tall[:, :, cols_here - deep :].reshape(-1), "sub", forward)
    from_right = lax.ppermute(tall[:, :, :deep].reshape(-1), "sub", backward)
    gap = jnp.zeros(tall.shape[:2] + (width - cols_here - 2 * deep,), jnp.float32)
    full = jnp.concatenate(
        [tall, from_right.reshape(edge_shape), gap, from_left.reshape(edge_shape)], axis=2
    )
    src_x = full[:nf]
    jd_x = full[nf : nf + nf * nf].reshape((nf, nf) + full.shape[1:])
    fw_x = full[nf + nf * nf :]

    tall_rows = rows_here + 2 * deep
    ext_rows = np.arange(tall_rows)
    ext_rows = np.where(ext_rows < rows_here + deep, ext_rows, ext_rows - tall_rows)

    def row_factor(row_step, count):
        rows = ext_rows[:count]
        here = np.floor_divide(rows, rows_here)
        there = np.floor_divide(rows + row_step, rows_here)
        face = np.minimum(here, there)
        cross_below = jnp.asarray((here != there) & (face < 0))
        cross_above = jnp.asarray((here != there) & (face >= 0))
        unit = jnp.ones((count,), jnp.float32)
        return jnp.where(cross_above, link_above * unit, jnp.where(cross_below, link_below * unit, unit))

    adjoint = src_x
    for iteration in range(ITERS):
        last = iteration == ITERS - 1
        out_rows = rows_here if last else tall_rows
        out_cols = cols_here if last else width
        centre = adjoint[:, :out_rows, :out_cols]
        jd = jd_x[:, :, :out_rows, :out_cols]
        fw = fw_x[:, :out_rows, :out_cols]
        src = src_x[:, :out_rows, :out_cols]
        result = centre + jnp.einsum("fgij,gij->fij", jd, centre, precision=lax.Precision.HIGHEST)
        for direction in range(len(offsets_table)):
            row_step, col_step = offsets_table[direction]
            shifted = jnp.roll(adjoint, (-row_step, -col_step), axis=(1, 2))[:, :out_rows, :out_cols]
            if row_step != 0:
                shifted = shifted * row_factor(row_step, out_rows)[None, :, None]
            mixed = jnp.einsum(
                "fg,gij->fij", flux_jac[direction], shifted, precision=lax.Precision.HIGHEST
            )
            result = result - fw[direction][None] * mixed
        adjoint = centre + relax_factor * (src - result)

    sensitivity = jnp.einsum(
        "cfij,fij->cij", node_grad.astype(jnp.float32), adjoint, precision=lax.Precision.HIGHEST
    )
    moved = lax.all_to_all(sensitivity, "sub", split_axis=1, concat_axis=2, tiled=True)

    part_axis = ("blk", "sub")
    part_index = block_index * sub_count + lax.axis_index("sub")
    part_count = block_count * sub_count
    warp_rows = moved.shape[1]
    both = jnp.concatenate([moved, stiffness[None]], axis=0)
    forward, backward = ring_pairs(part_count, False)
    part_below = lax.ppermute(both, part_axis, forward)
    part_above = lax.ppermute(both, part_axis, backward)
    both_x = jnp.concatenate([both, part_above, part_below], axis=1)
    local_rows = np.arange(3 * warp_rows)
    local_rows = np.where(local_rows < 2 * warp_rows, local_rows, local_rows - 3 * warp_rows)
    global_rows = part_index * warp_rows + jnp.asarray(local_rows, jnp.int32)
    valid = ((global_rows >= 0) & (global_rows < part_count * warp_rows))[:, None]
    sens_x = both_x[:-1]
    stiff_x = jnp.where(valid, both_x[-1], 1.0)
    root_stiff = jnp.sqrt(stiff_x)
    base_term = sens_x / stiff_x[None]
    scale_term = couple_factor / root_stiff
    warp_adjoint = jnp.zeros_like(base_term)
    for sweep_index in range(SWEEPS):
        spread = jnp.where(valid[None], root_stiff[None] * warp_adjoint, 0.0)
        beside_all = (
            jnp.roll(spread, 1, 1) + jnp.roll(spread, -1, 1) + jnp.roll(spread, 1, 2) + jnp.roll(spread, -1, 2)
        )
        warp_adjoint = base_term + scale_term[None] * beside_all
    return (adjoint, warp_adjoint[:, :warp_rows])


def solution(mesh):
    placed = (
        P(None, "blk", "sub"),
        P(None, None, "blk", "sub"),
        P(None, "blk", "sub"),
        P(),
        P(),
        P(None, None, "blk", "sub"),
        P(("blk", "sub"), None),
    )
    return jax.shard_map(
        local,
        mesh=mesh,
        in_specs=placed,
        out_specs=(P(None, "blk", "sub"), P(None, ("blk", "sub"), None)),
        check_vma=False,
    )
```

```python
import numpy as np
import jax
import jax.numpy as jnp
from jax import lax
from jax.sharding import PartitionSpec as P
from jax.experimental import pallas as pl
from jax.experimental.pallas import tpu as pltpu

ITERS = 4
SWEEPS = 6


relax_factor = 0.8
couple_factor = 2.0 / 9.0
offsets_table = ((1, 0), (-1, 0), (2, 0), (-2, 0), (0, 1), (0, -1), (0, 2), (0, -2))
REACH = 2
LANES = 128


def ring_pairs(count, periodic):
    forward = [(i, i + 1) for i in range(count - 1)]
    if periodic:
        forward.append((count - 1, 0))
    backward = [(target, source) for source, target in forward]
    return forward, backward


TILE = 8


def flow_kernel(flux_ref, link_ref, tile_ref, out_ref, buf0, buf1):
    nf = out_ref.shape[0]
    rows_here = out_ref.shape[1]
    cols_here = out_ref.shape[2]
    width = tile_ref.shape[2]
    pad = 2 * TILE
    n_tiles = tile_ref.shape[1] // TILE
    jd0 = nf
    fw0 = nf + nf * nf
    link_above = link_ref[0]
    link_below = link_ref[1]
    bufs = (buf0, buf1)
    for iteration in range(ITERS):
        pin = tile_ref if iteration == 0 else bufs[(iteration - 1) % 2]
        pout = bufs[iteration % 2]
        last = iteration == ITERS - 1
        first = pad // TILE if last else 1
        stop = (pad + rows_here) // TILE if last else n_tiles - 1

        def body(t, carry, pin=pin, pout=pout):
            r0 = pl.multiple_of(t * TILE, TILE)
            win = [pin[g, pl.ds(r0 - TILE, 3 * TILE), :] for g in range(nf)]
            centre = [w[TILE : 2 * TILE] for w in win]
            rows = r0 - pad + lax.broadcasted_iota(jnp.int32, (TILE, width), 0)
            here = (rows + 2 * rows_here) // rows_here
            acc = []
            for f in range(nf):
                a = tile_ref[jd0 + f * nf, pl.ds(r0, TILE), :] * centre[0]
                for g in range(1, nf):
                    a = a + tile_ref[jd0 + f * nf + g, pl.ds(r0, TILE), :] * centre[g]
                acc.append(centre[f] + a)
            for direction in range(len(offsets_table)):
                row_step, col_step = offsets_table[direction]
                if row_step != 0:
                    shifted = [
                        pltpu.roll(w, (-row_step) % (3 * TILE), 0)[TILE : 2 * TILE] for w in win
                    ]
                    there = (rows + row_step + 2 * rows_here) // rows_here
                    link = jnp.where(jnp.minimum(here, there) < 2, link_below, link_above)
                    factor = jnp.where(here != there, link, 1.0)
                    shifted = [x * factor for x in shifted]
                else:
                    shifted = [pltpu.roll(c, (-col_step) % width, 1) for c in centre]
                weight = tile_ref[fw0 + direction, pl.ds(r0, TILE), :]
                for f in range(nf):
                    base = direction * nf * nf + f * nf
                    mixed = flux_ref[base] * shifted[0]
                    for g in range(1, nf):
                        mixed = mixed + flux_ref[base + g] * shifted[g]
                    acc[f] = acc[f] - weight * mixed
            for f in range(nf):
                src = tile_ref[f, pl.ds(r0, TILE), :]
                pout[f, pl.ds(r0, TILE), :] = centre[f] + relax_factor * (src - acc[f])
            return carry

        lax.fori_loop(first, stop, body, 0)
    final = bufs[(ITERS - 1) % 2]
    out_ref[...] = final[:, pad : pad + rows_here, 0:cols_here]


def flow_iterations(flux_flat, links, tile, nf, rows_here, cols_here):
    return pl.pallas_call(
        flow_kernel,
        out_shape=jax.ShapeDtypeStruct((nf, rows_here, cols_here), jnp.float32),
        in_specs=[
            pl.BlockSpec(memory_space=pltpu.SMEM),
            pl.BlockSpec(memory_space=pltpu.SMEM),
            pl.BlockSpec(memory_space=pltpu.VMEM),
        ],
        out_specs=pl.BlockSpec(memory_space=pltpu.VMEM),
        scratch_shapes=[pltpu.VMEM((nf,) + tile.shape[1:], jnp.float32)] * 2,
        compiler_params=pltpu.CompilerParams(vmem_limit_bytes=48 * 1024 * 1024),
    )(flux_flat, links, tile)


def local(adj_source, jac_diag, face_weights, flux_jac, face_link, node_grad, stiffness):
    block_index = lax.axis_index("blk")
    block_count = lax.axis_size("blk")
    link_above = face_link[block_index].astype(jnp.float32)
    link_below = face_link[(block_index + block_count - 1) % block_count].astype(jnp.float32)
    nf = adj_source.shape[0]
    rows_here = adj_source.shape[1]
    cols_here = adj_source.shape[2]
    deep = REACH * ITERS
    width = -(-(cols_here + 2 * deep) // LANES) * LANES

    stack = jnp.concatenate(
        [adj_source, jac_diag.reshape((nf * nf,) + jac_diag.shape[2:]), face_weights], axis=0
    )
    forward, backward = ring_pairs(block_count, True)
    from_below = lax.ppermute(stack[:, rows_here - deep :], "blk", forward)
    from_above = lax.ppermute(stack[:, :deep], "blk", backward)
    zero_rows = jnp.zeros((stack.shape[0], 2 * TILE - deep, cols_here), jnp.float32)
    tall = jnp.concatenate([zero_rows, from_below, stack, from_above, zero_rows], axis=1)
    sub_count = lax.axis_size("sub")
    forward, backward = ring_pairs(sub_count, True)
    from_left = lax.ppermute(jnp.swapaxes(tall[:, :, cols_here - deep :], 1, 2), "sub", forward)
    from_right = lax.ppermute(jnp.swapaxes(tall[:, :, :deep], 1, 2), "sub", backward)
    gap = jnp.zeros(tall.shape[:2] + (width - cols_here - 2 * deep,), jnp.float32)
    tile = jnp.concatenate(
        [tall, jnp.swapaxes(from_right, 1, 2), gap, jnp.swapaxes(from_left, 1, 2)], axis=2
    )
    links = jnp.stack([link_above, link_below])
    adjoint = flow_iterations(flux_jac.reshape(-1), links, tile, nf, rows_here, cols_here)

    sensitivity = jnp.einsum(
        "cfij,fij->cij", node_grad.astype(jnp.float32), adjoint, precision=lax.Precision.HIGHEST
    )
    moved = lax.all_to_all(sensitivity, "sub", split_axis=1, concat_axis=2, tiled=True)

    part_axis = ("blk", "sub")
    part_index = block_index * sub_count + lax.axis_index("sub")
    part_count = block_count * sub_count
    warp_rows = moved.shape[1]
    both = jnp.concatenate([moved, stiffness[None]], axis=0)
    forward, backward = ring_pairs(part_count, False)
    part_below = lax.ppermute(both, part_axis, forward)
    part_above = lax.ppermute(both, part_axis, backward)
    both_x = jnp.concatenate([both, part_above, part_below], axis=1)
    local_rows = np.arange(3 * warp_rows)
    local_rows = np.where(local_rows < 2 * warp_rows, local_rows, local_rows - 3 * warp_rows)
    global_rows = part_index * warp_rows + jnp.asarray(local_rows, jnp.int32)
    valid = ((global_rows >= 0) & (global_rows < part_count * warp_rows))[:, None]
    sens_x = both_x[:-1]
    stiff_x = jnp.where(valid, both_x[-1], 1.0)
    root_stiff = jnp.sqrt(stiff_x)
    base_term = sens_x / stiff_x[None]
    scale_term = couple_factor / root_stiff
    warp_adjoint = jnp.zeros_like(base_term)
    for sweep_index in range(SWEEPS):
        spread = jnp.where(valid[None], root_stiff[None] * warp_adjoint, 0.0)
        beside_all = (
            jnp.roll(spread, 1, 1) + jnp.roll(spread, -1, 1) + jnp.roll(spread, 1, 2) + jnp.roll(spread, -1, 2)
        )
        warp_adjoint = base_term + scale_term[None] * beside_all
    return (adjoint, warp_adjoint[:, :warp_rows])


def solution(mesh):
    placed = (
        P(None, "blk", "sub"),
        P(None, None, "blk", "sub"),
        P(None, "blk", "sub"),
        P(),
        P(),
        P(None, None, "blk", "sub"),
        P(("blk", "sub"), None),
    )
    return jax.shard_map(
        local,
        mesh=mesh,
        in_specs=placed,
        out_specs=(P(None, "blk", "sub"), P(None, ("blk", "sub"), None)),
        check_vma=False,
    )
```

```python
import numpy as np
import jax
import jax.numpy as jnp
from jax import lax
from jax.sharding import PartitionSpec as P
from jax.experimental import pallas as pl
from jax.experimental.pallas import tpu as pltpu

ITERS = 4
SWEEPS = 6


relax_factor = 0.8
couple_factor = 2.0 / 9.0
offsets_table = ((1, 0), (-1, 0), (2, 0), (-2, 0), (0, 1), (0, -1), (0, 2), (0, -2))
REACH = 2
LANES = 128


def ring_pairs(count, periodic):
    forward = [(i, i + 1) for i in range(count - 1)]
    if periodic:
        forward.append((count - 1, 0))
    backward = [(target, source) for source, target in forward]
    return forward, backward


TILE = 8


def flow_kernel(flux_ref, link_ref, tile_ref, out_ref, buf0, buf1):
    nf = out_ref.shape[0]
    rows_here = out_ref.shape[1]
    cols_here = out_ref.shape[2]
    width = tile_ref.shape[2]
    pad = 2 * TILE
    n_tiles = tile_ref.shape[1] // TILE
    jd0 = nf
    fw0 = nf + nf * nf
    link_above = link_ref[0]
    link_below = link_ref[1]
    bufs = (buf0, buf1)
    for iteration in range(ITERS):
        pin = tile_ref if iteration == 0 else bufs[(iteration - 1) % 2]
        pout = bufs[iteration % 2]
        last = iteration == ITERS - 1
        first = pad // TILE if last else 1
        stop = (pad + rows_here) // TILE if last else n_tiles - 1

        def body(t, carry, pin=pin, pout=pout):
            r0 = pl.multiple_of(t * TILE, TILE)
            win = [pin[g, pl.ds(r0 - TILE, 3 * TILE), :] for g in range(nf)]
            centre = [w[TILE : 2 * TILE] for w in win]
            rows = r0 - pad + lax.broadcasted_iota(jnp.int32, (TILE, width), 0)
            here = (rows + 2 * rows_here) // rows_here
            acc = []
            for f in range(nf):
                a = tile_ref[jd0 + f * nf, pl.ds(r0, TILE), :] * centre[0]
                for g in range(1, nf):
                    a = a + tile_ref[jd0 + f * nf + g, pl.ds(r0, TILE), :] * centre[g]
                acc.append(centre[f] + a)
            for direction in range(len(offsets_table)):
                row_step, col_step = offsets_table[direction]
                if row_step != 0:
                    shifted = [
                        pltpu.roll(w, (-row_step) % (3 * TILE), 0)[TILE : 2 * TILE] for w in win
                    ]
                    there = (rows + row_step + 2 * rows_here) // rows_here
                    link = jnp.where(jnp.minimum(here, there) < 2, link_below, link_above)
                    factor = jnp.where(here != there, link, 1.0)
                    shifted = [x * factor for x in shifted]
                else:
                    shifted = [pltpu.roll(c, (-col_step) % width, 1) for c in centre]
                weight = tile_ref[fw0 + direction, pl.ds(r0, TILE), :]
                for f in range(nf):
                    base = direction * nf * nf + f * nf
                    mixed = flux_ref[base] * shifted[0]
                    for g in range(1, nf):
                        mixed = mixed + flux_ref[base + g] * shifted[g]
                    acc[f] = acc[f] - weight * mixed
            for f in range(nf):
                src = tile_ref[f, pl.ds(r0, TILE), :]
                pout[f, pl.ds(r0, TILE), :] = centre[f] + relax_factor * (src - acc[f])
            return carry

        lax.fori_loop(first, stop, body, 0)
    final = bufs[(ITERS - 1) % 2]
    out_ref[...] = final[:, pad : pad + rows_here, 0:cols_here]


def flow_iterations(flux_flat, links, tile, nf, rows_here, cols_here):
    return pl.pallas_call(
        flow_kernel,
        out_shape=jax.ShapeDtypeStruct((nf, rows_here, cols_here), jnp.float32),
        in_specs=[
            pl.BlockSpec(memory_space=pltpu.SMEM),
            pl.BlockSpec(memory_space=pltpu.SMEM),
            pl.BlockSpec(memory_space=pltpu.VMEM),
        ],
        out_specs=pl.BlockSpec(memory_space=pltpu.VMEM),
        scratch_shapes=[pltpu.VMEM((nf,) + tile.shape[1:], jnp.float32)] * 2,
        compiler_params=pltpu.CompilerParams(vmem_limit_bytes=48 * 1024 * 1024),
    )(flux_flat, links, tile)


def local(adj_source, jac_diag, face_weights, flux_jac, face_link, node_grad, stiffness):
    block_index = lax.axis_index("blk")
    block_count = lax.axis_size("blk")
    link_above = face_link[block_index].astype(jnp.float32)
    link_below = face_link[(block_index + block_count - 1) % block_count].astype(jnp.float32)
    nf = adj_source.shape[0]
    rows_here = adj_source.shape[1]
    cols_here = adj_source.shape[2]
    deep = REACH * ITERS
    width = -(-(cols_here + 2 * deep) // LANES) * LANES

    stack = jnp.concatenate(
        [adj_source, jac_diag.reshape((nf * nf,) + jac_diag.shape[2:]), face_weights], axis=0
    )
    sub_count = lax.axis_size("sub")

    def send(piece, row_move, col_move):
        pairs = [
            (b * sub_count + c, ((b + row_move) % block_count) * sub_count + (c + col_move) % sub_count)
            for b in range(block_count)
            for c in range(sub_count)
        ]
        return lax.ppermute(piece, ("blk", "sub"), pairs)

    low_rows = stack[:, rows_here - deep :]
    high_rows = stack[:, :deep]
    from_below = send(low_rows, 1, 0)
    from_above = send(high_rows, -1, 0)
    from_left = jnp.swapaxes(send(jnp.swapaxes(stack[:, :, cols_here - deep :], 1, 2), 0, 1), 1, 2)
    from_right = jnp.swapaxes(send(jnp.swapaxes(stack[:, :, :deep], 1, 2), 0, -1), 1, 2)
    below_left = send(low_rows[:, :, cols_here - deep :], 1, 1)
    below_right = send(low_rows[:, :, :deep], 1, -1)
    above_left = send(high_rows[:, :, cols_here - deep :], -1, 1)
    above_right = send(high_rows[:, :, :deep], -1, -1)
    zero_rows = jnp.zeros((stack.shape[0], 2 * TILE - deep, cols_here), jnp.float32)
    zero_strip = zero_rows[:, :, :deep]
    tall = jnp.concatenate([zero_rows, from_below, stack, from_above, zero_rows], axis=1)
    right = jnp.concatenate([zero_strip, below_right, from_right, above_right, zero_strip], axis=1)
    left = jnp.concatenate([zero_strip, below_left, from_left, above_left, zero_strip], axis=1)
    gap = jnp.zeros(tall.shape[:2] + (width - cols_here - 2 * deep,), jnp.float32)
    tile = jnp.concatenate([tall, right, gap, left], axis=2)
    links = jnp.stack([link_above, link_below])
    adjoint = flow_iterations(flux_jac.reshape(-1), links, tile, nf, rows_here, cols_here)

    sensitivity = jnp.einsum(
        "cfij,fij->cij", node_grad.astype(jnp.float32), adjoint, precision=lax.Precision.HIGHEST
    )
    moved = lax.all_to_all(sensitivity, "sub", split_axis=1, concat_axis=2, tiled=True)

    part_axis = ("blk", "sub")
    part_index = block_index * sub_count + lax.axis_index("sub")
    part_count = block_count * sub_count
    warp_rows = moved.shape[1]
    both = jnp.concatenate([moved, stiffness[None]], axis=0)
    forward, backward = ring_pairs(part_count, False)
    part_below = lax.ppermute(both, part_axis, forward)
    part_above = lax.ppermute(both, part_axis, backward)
    both_x = jnp.concatenate([both, part_above, part_below], axis=1)
    local_rows = np.arange(3 * warp_rows)
    local_rows = np.where(local_rows < 2 * warp_rows, local_rows, local_rows - 3 * warp_rows)
    global_rows = part_index * warp_rows + jnp.asarray(local_rows, jnp.int32)
    valid = ((global_rows >= 0) & (global_rows < part_count * warp_rows))[:, None]
    sens_x = both_x[:-1]
    stiff_x = jnp.where(valid, both_x[-1], 1.0)
    root_stiff = jnp.sqrt(stiff_x)
    base_term = sens_x / stiff_x[None]
    scale_term = couple_factor / root_stiff
    warp_adjoint = jnp.zeros_like(base_term)
    for sweep_index in range(SWEEPS):
        spread = jnp.where(valid[None], root_stiff[None] * warp_adjoint, 0.0)
        beside_all = (
            jnp.roll(spread, 1, 1) + jnp.roll(spread, -1, 1) + jnp.roll(spread, 1, 2) + jnp.roll(spread, -1, 2)
        )
        warp_adjoint = base_term + scale_term[None] * beside_all
    return (adjoint, warp_adjoint[:, :warp_rows])


def solution(mesh):
    placed = (
        P(None, "blk", "sub"),
        P(None, None, "blk", "sub"),
        P(None, "blk", "sub"),
        P(),
        P(),
        P(None, None, "blk", "sub"),
        P(("blk", "sub"), None),
    )
    return jax.shard_map(
        local,
        mesh=mesh,
        in_specs=placed,
        out_specs=(P(None, "blk", "sub"), P(None, ("blk", "sub"), None)),
        check_vma=False,
    )
```

```python
import functools
import numpy as np
import jax
import jax.numpy as jnp
from jax import lax
from jax.sharding import PartitionSpec as P
from jax.experimental import pallas as pl
from jax.experimental.pallas import tpu as pltpu

ITERS = 4
SWEEPS = 6


relax_factor = 0.8
couple_factor = 2.0 / 9.0
offsets_table = ((1, 0), (-1, 0), (2, 0), (-2, 0), (0, 1), (0, -1), (0, 2), (0, -2))
REACH = 2
LANES = 128


def ring_pairs(count, periodic):
    forward = [(i, i + 1) for i in range(count - 1)]
    if periodic:
        forward.append((count - 1, 0))
    backward = [(target, source) for source, target in forward]
    return forward, backward


TILE = 8


def flow_kernel(flux_ref, link_ref, tile_ref, out_ref, buf0, buf1):
    nf = out_ref.shape[0]
    rows_here = out_ref.shape[1]
    cols_here = out_ref.shape[2]
    width = tile_ref.shape[2]
    pad = 2 * TILE
    n_tiles = tile_ref.shape[1] // TILE
    jd0 = nf
    fw0 = nf + nf * nf
    link_above = link_ref[0]
    link_below = link_ref[1]
    bufs = (buf0, buf1)
    for iteration in range(ITERS):
        pin = tile_ref if iteration == 0 else bufs[(iteration - 1) % 2]
        pout = bufs[iteration % 2]
        last = iteration == ITERS - 1
        first = pad // TILE if last else 1
        stop = (pad + rows_here) // TILE if last else n_tiles - 1

        def body(t, carry, pin=pin, pout=pout):
            r0 = pl.multiple_of(t * TILE, TILE)
            win = [pin[g, pl.ds(r0 - TILE, 3 * TILE), :] for g in range(nf)]
            centre = [w[TILE : 2 * TILE] for w in win]
            rows = r0 - pad + lax.broadcasted_iota(jnp.int32, (TILE, width), 0)
            here = (rows + 2 * rows_here) // rows_here
            acc = []
            for f in range(nf):
                a = tile_ref[jd0 + f * nf, pl.ds(r0, TILE), :] * centre[0]
                for g in range(1, nf):
                    a = a + tile_ref[jd0 + f * nf + g, pl.ds(r0, TILE), :] * centre[g]
                acc.append(centre[f] + a)
            for direction in range(len(offsets_table)):
                row_step, col_step = offsets_table[direction]
                if row_step != 0:
                    shifted = [
                        pltpu.roll(w, (-row_step) % (3 * TILE), 0)[TILE : 2 * TILE] for w in win
                    ]
                    there = (rows + row_step + 2 * rows_here) // rows_here
                    link = jnp.where(jnp.minimum(here, there) < 2, link_below, link_above)
                    factor = jnp.where(here != there, link, 1.0)
                    shifted = [x * factor for x in shifted]
                else:
                    shifted = [pltpu.roll(c, (-col_step) % width, 1) for c in centre]
                weight = tile_ref[fw0 + direction, pl.ds(r0, TILE), :]
                for f in range(nf):
                    base = direction * nf * nf + f * nf
                    mixed = flux_ref[base] * shifted[0]
                    for g in range(1, nf):
                        mixed = mixed + flux_ref[base + g] * shifted[g]
                    acc[f] = acc[f] - weight * mixed
            for f in range(nf):
                src = tile_ref[f, pl.ds(r0, TILE), :]
                pout[f, pl.ds(r0, TILE), :] = centre[f] + relax_factor * (src - acc[f])
            return carry

        lax.fori_loop(first, stop, body, 0)
    final = bufs[(ITERS - 1) % 2]
    out_ref[...] = final[:, pad : pad + rows_here, 0:cols_here]


def flow_iterations(flux_flat, links, tile, nf, rows_here, cols_here):
    return pl.pallas_call(
        flow_kernel,
        out_shape=jax.ShapeDtypeStruct((nf, rows_here, cols_here), jnp.float32),
        in_specs=[
            pl.BlockSpec(memory_space=pltpu.SMEM),
            pl.BlockSpec(memory_space=pltpu.SMEM),
            pl.BlockSpec(memory_space=pltpu.VMEM),
        ],
        out_specs=pl.BlockSpec(memory_space=pltpu.VMEM),
        scratch_shapes=[pltpu.VMEM((nf,) + tile.shape[1:], jnp.float32)] * 2,
        compiler_params=pltpu.CompilerParams(vmem_limit_bytes=48 * 1024 * 1024),
    )(flux_flat, links, tile)


def local(adj_source, jac_diag, face_weights, flux_jac, face_link, node_grad, stiffness):
    block_index = lax.axis_index("blk")
    block_count = lax.axis_size("blk")
    link_above = face_link[block_index].astype(jnp.float32)
    link_below = face_link[(block_index + block_count - 1) % block_count].astype(jnp.float32)
    nf = adj_source.shape[0]
    rows_here = adj_source.shape[1]
    cols_here = adj_source.shape[2]
    deep = REACH * ITERS
    width = -(-(cols_here + 2 * deep) // LANES) * LANES

    stack = jnp.concatenate(
        [adj_source, jac_diag.reshape((nf * nf,) + jac_diag.shape[2:]), face_weights], axis=0
    )
    forward, backward = ring_pairs(block_count, True)
    from_below = lax.ppermute(stack[:, rows_here - deep :], "blk", forward)
    from_above = lax.ppermute(stack[:, :deep], "blk", backward)
    zero_rows = jnp.zeros((stack.shape[0], 2 * TILE - deep, cols_here), jnp.float32)
    tall = jnp.concatenate([zero_rows, from_below, stack, from_above, zero_rows], axis=1)
    sub_count = lax.axis_size("sub")
    forward, backward = ring_pairs(sub_count, True)
    from_left = lax.ppermute(jnp.swapaxes(tall[:, :, cols_here - deep :], 1, 2), "sub", forward)
    from_right = lax.ppermute(jnp.swapaxes(tall[:, :, :deep], 1, 2), "sub", backward)
    gap = jnp.zeros(tall.shape[:2] + (width - cols_here - 2 * deep,), jnp.float32)
    tile = jnp.concatenate(
        [tall, jnp.swapaxes(from_right, 1, 2), gap, jnp.swapaxes(from_left, 1, 2)], axis=2
    )
    links = jnp.stack([link_above, link_below])
    adjoint = flow_iterations(flux_jac.reshape(-1), links, tile, nf, rows_here, cols_here)

    sensitivity = jnp.einsum(
        "cfij,fij->cij", node_grad.astype(jnp.float32), adjoint, precision=lax.Precision.HIGHEST
    )
    moved = lax.all_to_all(sensitivity, "sub", split_axis=1, concat_axis=2, tiled=True)

    part_axis = ("blk", "sub")
    part_index = block_index * sub_count + lax.axis_index("sub")
    part_count = block_count * sub_count
    warp_rows = moved.shape[1]
    both = jnp.concatenate([moved, stiffness[None]], axis=0)
    forward, backward = ring_pairs(part_count, False)
    part_below = lax.ppermute(both, part_axis, forward)
    part_above = lax.ppermute(both, part_axis, backward)
    warp_adjoint = warp_sweeps(part_index.reshape(1), both, part_above, part_below, part_count)
    return (adjoint, warp_adjoint)


def warp_kernel(part_count, index_ref, mid_ref, above_ref, below_ref, out_ref):
    ncomp = out_ref.shape[0]
    warp_rows = out_ref.shape[1]
    cols = out_ref.shape[2]
    tall_rows = 3 * warp_rows
    rows = lax.broadcasted_iota(jnp.int32, (tall_rows, cols), 0)
    local_rows = jnp.where(rows < 2 * warp_rows, rows, rows - tall_rows)
    global_rows = index_ref[0] * warp_rows + local_rows
    valid = (global_rows >= 0) & (global_rows < part_count * warp_rows)

    def field(c):
        return jnp.concatenate([mid_ref[c], above_ref[c], below_ref[c]], axis=0)

    stiff = jnp.where(valid, field(ncomp), 1.0)
    root_stiff = jnp.sqrt(stiff)
    scale_term = couple_factor / root_stiff
    base_term = [field(c) / stiff for c in range(ncomp)]
    warp = [jnp.zeros((tall_rows, cols), jnp.float32) for c in range(ncomp)]
    for sweep_index in range(SWEEPS):
        for c in range(ncomp):
            spread = jnp.where(valid, root_stiff * warp[c], 0.0)
            beside_all = (
                pltpu.roll(spread, 1, 0)
                + pltpu.roll(spread, tall_rows - 1, 0)
                + pltpu.roll(spread, 1, 1)
                + pltpu.roll(spread, cols - 1, 1)
            )
            warp[c] = base_term[c] + scale_term * beside_all
    for c in range(ncomp):
        out_ref[c] = warp[c][:warp_rows]


def warp_sweeps(index, mid, above, below, part_count):
    ncomp = mid.shape[0] - 1
    return pl.pallas_call(
        functools.partial(warp_kernel, part_count),
        out_shape=jax.ShapeDtypeStruct((ncomp,) + mid.shape[1:], jnp.float32),
        in_specs=[pl.BlockSpec(memory_space=pltpu.SMEM)]
        + [pl.BlockSpec(memory_space=pltpu.VMEM)] * 3,
        out_specs=pl.BlockSpec(memory_space=pltpu.VMEM),
    )(index, mid, above, below)


def solution(mesh):
    placed = (
        P(None, "blk", "sub"),
        P(None, None, "blk", "sub"),
        P(None, "blk", "sub"),
        P(),
        P(),
        P(None, None, "blk", "sub"),
        P(("blk", "sub"), None),
    )
    return jax.shard_map(
        local,
        mesh=mesh,
        in_specs=placed,
        out_specs=(P(None, "blk", "sub"), P(None, ("blk", "sub"), None)),
        check_vma=False,
    )
```

```python
import functools
import numpy as np
import jax
import jax.numpy as jnp
from jax import lax
from jax.sharding import PartitionSpec as P
from jax.experimental import pallas as pl
from jax.experimental.pallas import tpu as pltpu

ITERS = 4
SWEEPS = 6


relax_factor = 0.8
couple_factor = 2.0 / 9.0
offsets_table = ((1, 0), (-1, 0), (2, 0), (-2, 0), (0, 1), (0, -1), (0, 2), (0, -2))
REACH = 2
LANES = 128


def ring_pairs(count, periodic):
    forward = [(i, i + 1) for i in range(count - 1)]
    if periodic:
        forward.append((count - 1, 0))
    backward = [(target, source) for source, target in forward]
    return forward, backward


TILE = 8


def flow_kernel(flux_ref, link_ref, adj_hbm, jd_hbm, fw_hbm, below_hbm, above_hbm, edge_hbm,
                out_ref, tile_ref, buf0, buf1, sems):
    nf = out_ref.shape[0]
    rows_here = out_ref.shape[1]
    cols_here = out_ref.shape[2]
    width = tile_ref.shape[2]
    pad = 2 * TILE
    halo = below_hbm.shape[1]
    n_fields = tile_ref.shape[0]
    n_tiles = tile_ref.shape[1] // TILE
    jd0 = nf
    fw0 = nf + nf * nf
    copies = [
        pltpu.make_async_copy(adj_hbm, tile_ref.at[0:jd0, pad : pad + rows_here, 0:cols_here], sems.at[0]),
        pltpu.make_async_copy(jd_hbm, tile_ref.at[jd0:fw0, pad : pad + rows_here, 0:cols_here], sems.at[1]),
        pltpu.make_async_copy(fw_hbm, tile_ref.at[fw0:n_fields, pad : pad + rows_here, 0:cols_here], sems.at[2]),
        pltpu.make_async_copy(below_hbm, tile_ref.at[:, pad - halo : pad, 0:cols_here], sems.at[3]),
        pltpu.make_async_copy(
            above_hbm, tile_ref.at[:, pad + rows_here : pad + rows_here + halo, 0:cols_here], sems.at[4]
        ),
        pltpu.make_async_copy(edge_hbm, tile_ref.at[:, :, cols_here:width], sems.at[5]),
    ]
    for copy in copies:
        copy.start()
    for copy in copies:
        copy.wait()
    zeros = jnp.zeros((n_fields, pad - halo, cols_here), jnp.float32)
    tile_ref[:, 0 : pad - halo, 0:cols_here] = zeros
    tile_ref[:, pad + rows_here + halo :, 0:cols_here] = zeros
    link_above = link_ref[0]
    link_below = link_ref[1]
    bufs = (buf0, buf1)
    for iteration in range(ITERS):
        pin = tile_ref if iteration == 0 else bufs[(iteration - 1) % 2]
        pout = bufs[iteration % 2]
        last = iteration == ITERS - 1
        first = pad // TILE if last else 1
        stop = (pad + rows_here) // TILE if last else n_tiles - 1

        def body(t, carry, pin=pin, pout=pout):
            r0 = pl.multiple_of(t * TILE, TILE)
            win = [pin[g, pl.ds(r0 - TILE, 3 * TILE), :] for g in range(nf)]
            centre = [w[TILE : 2 * TILE] for w in win]
            rows = r0 - pad + lax.broadcasted_iota(jnp.int32, (TILE, width), 0)
            here = (rows + 2 * rows_here) // rows_here
            acc = []
            for f in range(nf):
                a = tile_ref[jd0 + f * nf, pl.ds(r0, TILE), :] * centre[0]
                for g in range(1, nf):
                    a = a + tile_ref[jd0 + f * nf + g, pl.ds(r0, TILE), :] * centre[g]
                acc.append(centre[f] + a)
            for direction in range(len(offsets_table)):
                row_step, col_step = offsets_table[direction]
                if row_step != 0:
                    shifted = [
                        pltpu.roll(w, (-row_step) % (3 * TILE), 0)[TILE : 2 * TILE] for w in win
                    ]
                    there = (rows + row_step + 2 * rows_here) // rows_here
                    link = jnp.where(jnp.minimum(here, there) < 2, link_below, link_above)
                    factor = jnp.where(here != there, link, 1.0)
                    shifted = [x * factor for x in shifted]
                else:
                    shifted = [pltpu.roll(c, (-col_step) % width, 1) for c in centre]
                weight = tile_ref[fw0 + direction, pl.ds(r0, TILE), :]
                for f in range(nf):
                    base = direction * nf * nf + f * nf
                    mixed = flux_ref[base] * shifted[0]
                    for g in range(1, nf):
                        mixed = mixed + flux_ref[base + g] * shifted[g]
                    acc[f] = acc[f] - weight * mixed
            for f in range(nf):
                src = tile_ref[f, pl.ds(r0, TILE), :]
                pout[f, pl.ds(r0, TILE), :] = centre[f] + relax_factor * (src - acc[f])
            return carry

        lax.fori_loop(first, stop, body, 0)
    final = bufs[(ITERS - 1) % 2]
    out_ref[...] = final[:, pad : pad + rows_here, 0:cols_here]


def flow_iterations(flux_flat, links, adj, jd, fw, below, above, edge, width):
    nf, rows_here, cols_here = adj.shape
    n_fields = below.shape[0]
    tile_shape = (n_fields, rows_here + 4 * TILE, width)
    return pl.pallas_call(
        flow_kernel,
        out_shape=jax.ShapeDtypeStruct((nf, rows_here, cols_here), jnp.float32),
        in_specs=[
            pl.BlockSpec(memory_space=pltpu.SMEM),
            pl.BlockSpec(memory_space=pltpu.SMEM),
        ]
        + [pl.BlockSpec(memory_space=pl.ANY)] * 6,
        out_specs=pl.BlockSpec(memory_space=pltpu.VMEM),
        scratch_shapes=[
            pltpu.VMEM(tile_shape, jnp.float32),
            pltpu.VMEM((nf,) + tile_shape[1:], jnp.float32),
            pltpu.VMEM((nf,) + tile_shape[1:], jnp.float32),
            pltpu.SemaphoreType.DMA((6,)),
        ],
        compiler_params=pltpu.CompilerParams(vmem_limit_bytes=48 * 1024 * 1024),
    )(flux_flat, links, adj, jd, fw, below, above, edge)


def local(adj_source, jac_diag, face_weights, flux_jac, face_link, node_grad, stiffness):
    block_index = lax.axis_index("blk")
    block_count = lax.axis_size("blk")
    link_above = face_link[block_index].astype(jnp.float32)
    link_below = face_link[(block_index + block_count - 1) % block_count].astype(jnp.float32)
    nf = adj_source.shape[0]
    rows_here = adj_source.shape[1]
    cols_here = adj_source.shape[2]
    deep = REACH * ITERS
    width = -(-(cols_here + 2 * deep) // LANES) * LANES

    fields = [adj_source, jac_diag.reshape((nf * nf,) + jac_diag.shape[2:]), face_weights]
    forward, backward = ring_pairs(block_count, True)
    from_below = lax.ppermute(
        jnp.concatenate([x[:, rows_here - deep :] for x in fields], axis=0), "blk", forward
    )
    from_above = lax.ppermute(jnp.concatenate([x[:, :deep] for x in fields], axis=0), "blk", backward)
    sub_count = lax.axis_size("sub")
    forward, backward = ring_pairs(sub_count, True)

    def column_strip(lo, hi):
        middle = jnp.concatenate([x[:, :, lo:hi] for x in fields], axis=0)
        strip = jnp.concatenate([from_below[:, :, lo:hi], middle, from_above[:, :, lo:hi]], axis=1)
        return jnp.swapaxes(strip, 1, 2)

    from_left = lax.ppermute(column_strip(cols_here - deep, cols_here), "sub", forward)
    from_right = lax.ppermute(column_strip(0, deep), "sub", backward)
    gap = jnp.zeros(from_left.shape[:1] + from_left.shape[2:] + (width - cols_here - 2 * deep,), jnp.float32)
    edge = jnp.concatenate([jnp.swapaxes(from_right, 1, 2), gap, jnp.swapaxes(from_left, 1, 2)], axis=2)
    edge = jnp.pad(edge, ((0, 0), (2 * TILE - deep, 2 * TILE - deep), (0, 0)))
    links = jnp.stack([link_above, link_below])
    adjoint = flow_iterations(
        flux_jac.reshape(-1), links, fields[0], fields[1], fields[2], from_below, from_above, edge, width
    )

    sensitivity = jnp.einsum(
        "cfij,fij->cij", node_grad.astype(jnp.float32), adjoint, precision=lax.Precision.HIGHEST
    )
    moved = lax.all_to_all(sensitivity, "sub", split_axis=1, concat_axis=2, tiled=True)

    part_axis = ("blk", "sub")
    part_index = block_index * sub_count + lax.axis_index("sub")
    part_count = block_count * sub_count
    warp_rows = moved.shape[1]
    both = jnp.concatenate([moved, stiffness[None]], axis=0)
    forward, backward = ring_pairs(part_count, False)
    part_below = lax.ppermute(both, part_axis, forward)
    part_above = lax.ppermute(both, part_axis, backward)
    warp_adjoint = warp_sweeps(part_index.reshape(1), both, part_above, part_below, part_count)
    return (adjoint, warp_adjoint)


def warp_kernel(part_count, index_ref, mid_ref, above_ref, below_ref, out_ref):
    ncomp = out_ref.shape[0]
    warp_rows = out_ref.shape[1]
    cols = out_ref.shape[2]
    tall_rows = 3 * warp_rows
    rows = lax.broadcasted_iota(jnp.int32, (tall_rows, cols), 0)
    local_rows = jnp.where(rows < 2 * warp_rows, rows, rows - tall_rows)
    global_rows = index_ref[0] * warp_rows + local_rows
    valid = (global_rows >= 0) & (global_rows < part_count * warp_rows)

    def field(c):
        return jnp.concatenate([mid_ref[c], above_ref[c], below_ref[c]], axis=0)

    stiff = jnp.where(valid, field(ncomp), 1.0)
    root_stiff = jnp.sqrt(stiff)
    scale_term = couple_factor / root_stiff
    base_term = [field(c) / stiff for c in range(ncomp)]
    warp = [jnp.zeros((tall_rows, cols), jnp.float32) for c in range(ncomp)]
    for sweep_index in range(SWEEPS):
        for c in range(ncomp):
            spread = jnp.where(valid, root_stiff * warp[c], 0.0)
            beside_all = (
                pltpu.roll(spread, 1, 0)
                + pltpu.roll(spread, tall_rows - 1, 0)
                + pltpu.roll(spread, 1, 1)
                + pltpu.roll(spread, cols - 1, 1)
            )
            warp[c] = base_term[c] + scale_term * beside_all
    for c in range(ncomp):
        out_ref[c] = warp[c][:warp_rows]


def warp_sweeps(index, mid, above, below, part_count):
    ncomp = mid.shape[0] - 1
    return pl.pallas_call(
        functools.partial(warp_kernel, part_count),
        out_shape=jax.ShapeDtypeStruct((ncomp,) + mid.shape[1:], jnp.float32),
        in_specs=[pl.BlockSpec(memory_space=pltpu.SMEM)]
        + [pl.BlockSpec(memory_space=pltpu.VMEM)] * 3,
        out_specs=pl.BlockSpec(memory_space=pltpu.VMEM),
    )(index, mid, above, below)


def solution(mesh):
    placed = (
        P(None, "blk", "sub"),
        P(None, None, "blk", "sub"),
        P(None, "blk", "sub"),
        P(),
        P(),
        P(None, None, "blk", "sub"),
        P(("blk", "sub"), None),
    )
    return jax.shard_map(
        local,
        mesh=mesh,
        in_specs=placed,
        out_specs=(P(None, "blk", "sub"), P(None, ("blk", "sub"), None)),
        check_vma=False,
    )
```

```python
import functools
import numpy as np
import jax
import jax.numpy as jnp
from jax import lax
from jax.sharding import PartitionSpec as P
from jax.experimental import pallas as pl
from jax.experimental.pallas import tpu as pltpu

ITERS = 4
SWEEPS = 6


relax_factor = 0.8
couple_factor = 2.0 / 9.0
offsets_table = ((1, 0), (-1, 0), (2, 0), (-2, 0), (0, 1), (0, -1), (0, 2), (0, -2))
REACH = 2
LANES = 128


def ring_pairs(count, periodic):
    forward = [(i, i + 1) for i in range(count - 1)]
    if periodic:
        forward.append((count - 1, 0))
    backward = [(target, source) for source, target in forward]
    return forward, backward


TILE = 8
STRIPS = 16


def pack_kernel(adj_lo, adj_hi, jd_lo, jd_hi, fw_lo, fw_hi, below_lo, below_hi, above_lo, above_hi,
                low_ref, high_ref):
    strip = low_ref.shape[2] // STRIPS
    lanes = low_ref.shape[2]
    lane = lax.broadcasted_iota(jnp.int32, low_ref.shape[1:], 1)
    low = [jnp.zeros(low_ref.shape[1:], jnp.float32) for _ in range(low_ref.shape[0])]
    high = [jnp.zeros(high_ref.shape[1:], jnp.float32) for _ in range(high_ref.shape[0])]
    index = 0
    for lo_ref, hi_ref in ((adj_lo, adj_hi), (jd_lo, jd_hi), (fw_lo, fw_hi)):
        for f in range(lo_ref.shape[0]):
            group, slot = divmod(index, STRIPS)
            lo = jnp.concatenate([below_lo[index], lo_ref[f], above_lo[index]], axis=0)
            hi = jnp.concatenate([below_hi[index], hi_ref[f], above_hi[index]], axis=0)
            keep = (lane >= strip * slot) & (lane < strip * (slot + 1))
            low[group] = jnp.where(keep, pltpu.roll(lo, (strip * slot) % lanes, 1), low[group])
            high[group] = jnp.where(
                keep, pltpu.roll(hi, (strip * slot - (lanes - strip)) % lanes, 1), high[group]
            )
            index += 1
    for group in range(low_ref.shape[0]):
        low_ref[group] = low[group]
        high_ref[group] = high[group]


def pack_strips(fields, below, above, deep):
    rows_here, cols_here = fields[0].shape[1:]
    n_fields = below.shape[0]
    groups = -(-n_fields // STRIPS)
    last = cols_here // LANES - 1

    def chunk(x, c):
        return pl.BlockSpec((x.shape[0], x.shape[1], LANES), lambda i: (0, 0, c))

    specs = []
    args = []
    for x in list(fields) + [below, above]:
        specs += [chunk(x, 0), chunk(x, last)]
        args += [x, x]
    out = jax.ShapeDtypeStruct((groups, rows_here + 2 * deep, LANES), jnp.float32)
    return pl.pallas_call(
        pack_kernel,
        out_shape=(out, out),
        grid=(1,),
        in_specs=specs,
        out_specs=(pl.BlockSpec(out.shape, lambda i: (0, 0, 0)),) * 2,
    )(*args)


def flow_kernel(flux_ref, link_ref, adj_hbm, jd_hbm, fw_hbm, below_hbm, above_hbm, left_ref, right_ref,
                out_ref, tile_ref, buf0, buf1, sems):
    nf = out_ref.shape[0]
    rows_here = out_ref.shape[1]
    cols_here = out_ref.shape[2]
    width = tile_ref.shape[2]
    pad = 2 * TILE
    halo = below_hbm.shape[1]
    n_fields = tile_ref.shape[0]
    n_tiles = tile_ref.shape[1] // TILE
    jd0 = nf
    fw0 = nf + nf * nf
    copies = [
        pltpu.make_async_copy(adj_hbm, tile_ref.at[0:jd0, pad : pad + rows_here, 0:cols_here], sems.at[0]),
        pltpu.make_async_copy(jd_hbm, tile_ref.at[jd0:fw0, pad : pad + rows_here, 0:cols_here], sems.at[1]),
        pltpu.make_async_copy(fw_hbm, tile_ref.at[fw0:n_fields, pad : pad + rows_here, 0:cols_here], sems.at[2]),
        pltpu.make_async_copy(below_hbm, tile_ref.at[:, pad - halo : pad, 0:cols_here], sems.at[3]),
        pltpu.make_async_copy(
            above_hbm, tile_ref.at[:, pad + rows_here : pad + rows_here + halo, 0:cols_here], sems.at[4]
        ),
    ]
    for copy in copies:
        copy.start()
    for copy in copies:
        copy.wait()
    zeros = jnp.zeros((n_fields, pad - halo, width), jnp.float32)
    tile_ref[:, 0 : pad - halo, :] = zeros
    tile_ref[:, pad + rows_here + halo :, :] = zeros
    lanes = width - cols_here
    strip = lanes // STRIPS
    lane = lax.broadcasted_iota(jnp.int32, left_ref.shape[1:], 1)
    for index in range(n_fields):
        group, slot = divmod(index, STRIPS)
        after = pltpu.roll(right_ref[group], (-strip * slot) % lanes, 1)
        before = pltpu.roll(left_ref[group], (lanes - strip - strip * slot) % lanes, 1)
        edge = jnp.where(lane < halo, after, jnp.where(lane >= lanes - halo, before, 0.0))
        tile_ref[index, pad - halo : pad + rows_here + halo, cols_here:width] = edge
    link_above = link_ref[0]
    link_below = link_ref[1]
    bufs = (buf0, buf1)
    for iteration in range(ITERS):
        pin = tile_ref if iteration == 0 else bufs[(iteration - 1) % 2]
        pout = bufs[iteration % 2]
        last = iteration == ITERS - 1
        first = pad // TILE if last else 1
        stop = (pad + rows_here) // TILE if last else n_tiles - 1

        def body(t, carry, pin=pin, pout=pout):
            r0 = pl.multiple_of(t * TILE, TILE)
            win = [pin[g, pl.ds(r0 - TILE, 3 * TILE), :] for g in range(nf)]
            centre = [w[TILE : 2 * TILE] for w in win]
            rows = r0 - pad + lax.broadcasted_iota(jnp.int32, (TILE, width), 0)
            here = (rows + 2 * rows_here) // rows_here
            acc = []
            for f in range(nf):
                a = tile_ref[jd0 + f * nf, pl.ds(r0, TILE), :] * centre[0]
                for g in range(1, nf):
                    a = a + tile_ref[jd0 + f * nf + g, pl.ds(r0, TILE), :] * centre[g]
                acc.append(centre[f] + a)
            for direction in range(len(offsets_table)):
                row_step, col_step = offsets_table[direction]
                if row_step != 0:
                    shifted = [
                        pltpu.roll(w, (-row_step) % (3 * TILE), 0)[TILE : 2 * TILE] for w in win
                    ]
                    there = (rows + row_step + 2 * rows_here) // rows_here
                    link = jnp.where(jnp.minimum(here, there) < 2, link_below, link_above)
                    factor = jnp.where(here != there, link, 1.0)
                    shifted = [x * factor for x in shifted]
                else:
                    shifted = [pltpu.roll(c, (-col_step) % width, 1) for c in centre]
                weight = tile_ref[fw0 + direction, pl.ds(r0, TILE), :]
                for f in range(nf):
                    base = direction * nf * nf + f * nf
                    mixed = flux_ref[base] * shifted[0]
                    for g in range(1, nf):
                        mixed = mixed + flux_ref[base + g] * shifted[g]
                    acc[f] = acc[f] - weight * mixed
            for f in range(nf):
                src = tile_ref[f, pl.ds(r0, TILE), :]
                pout[f, pl.ds(r0, TILE), :] = centre[f] + relax_factor * (src - acc[f])
            return carry

        lax.fori_loop(first, stop, body, 0)
    final = bufs[(ITERS - 1) % 2]
    out_ref[...] = final[:, pad : pad + rows_here, 0:cols_here]


def flow_iterations(flux_flat, links, adj, jd, fw, below, above, left, right, width):
    nf, rows_here, cols_here = adj.shape
    n_fields = below.shape[0]
    tile_shape = (n_fields, rows_here + 4 * TILE, width)
    return pl.pallas_call(
        flow_kernel,
        out_shape=jax.ShapeDtypeStruct((nf, rows_here, cols_here), jnp.float32),
        in_specs=[
            pl.BlockSpec(memory_space=pltpu.SMEM),
            pl.BlockSpec(memory_space=pltpu.SMEM),
        ]
        + [pl.BlockSpec(memory_space=pl.ANY)] * 5
        + [pl.BlockSpec(memory_space=pltpu.VMEM)] * 2,
        out_specs=pl.BlockSpec(memory_space=pltpu.VMEM),
        scratch_shapes=[
            pltpu.VMEM(tile_shape, jnp.float32),
            pltpu.VMEM((nf,) + tile_shape[1:], jnp.float32),
            pltpu.VMEM((nf,) + tile_shape[1:], jnp.float32),
            pltpu.SemaphoreType.DMA((5,)),
        ],
        compiler_params=pltpu.CompilerParams(vmem_limit_bytes=48 * 1024 * 1024),
    )(flux_flat, links, adj, jd, fw, below, above, left, right)


def local(adj_source, jac_diag, face_weights, flux_jac, face_link, node_grad, stiffness):
    block_index = lax.axis_index("blk")
    block_count = lax.axis_size("blk")
    link_above = face_link[block_index].astype(jnp.float32)
    link_below = face_link[(block_index + block_count - 1) % block_count].astype(jnp.float32)
    nf = adj_source.shape[0]
    rows_here = adj_source.shape[1]
    cols_here = adj_source.shape[2]
    deep = REACH * ITERS
    width = -(-(cols_here + 2 * deep) // LANES) * LANES

    fields = [adj_source, jac_diag.reshape((nf * nf,) + jac_diag.shape[2:]), face_weights]
    forward, backward = ring_pairs(block_count, True)
    from_below = lax.ppermute(
        jnp.concatenate([x[:, rows_here - deep :] for x in fields], axis=0), "blk", forward
    )
    from_above = lax.ppermute(jnp.concatenate([x[:, :deep] for x in fields], axis=0), "blk", backward)
    sub_count = lax.axis_size("sub")
    forward, backward = ring_pairs(sub_count, True)

    low_strips, high_strips = pack_strips(fields, from_below, from_above, deep)
    from_left = lax.ppermute(high_strips, "sub", forward)
    from_right = lax.ppermute(low_strips, "sub", backward)
    links = jnp.stack([link_above, link_below])
    adjoint = flow_iterations(
        flux_jac.reshape(-1), links, fields[0], fields[1], fields[2], from_below, from_above,
        from_left, from_right, width
    )

    sensitivity = jnp.einsum(
        "cfij,fij->cij", node_grad.astype(jnp.float32), adjoint, precision=lax.Precision.HIGHEST
    )
    moved = lax.all_to_all(sensitivity, "sub", split_axis=1, concat_axis=2, tiled=True)

    part_axis = ("blk", "sub")
    part_index = block_index * sub_count + lax.axis_index("sub")
    part_count = block_count * sub_count
    warp_rows = moved.shape[1]
    both = jnp.concatenate([moved, stiffness[None]], axis=0)
    forward, backward = ring_pairs(part_count, False)
    part_below = lax.ppermute(both, part_axis, forward)
    part_above = lax.ppermute(both, part_axis, backward)
    warp_adjoint = warp_sweeps(part_index.reshape(1), both, part_above, part_below, part_count)
    return (adjoint, warp_adjoint)


def warp_kernel(part_count, index_ref, mid_ref, above_ref, below_ref, out_ref):
    ncomp = out_ref.shape[0]
    warp_rows = out_ref.shape[1]
    cols = out_ref.shape[2]
    tall_rows = 3 * warp_rows
    rows = lax.broadcasted_iota(jnp.int32, (tall_rows, cols), 0)
    local_rows = jnp.where(rows < 2 * warp_rows, rows, rows - tall_rows)
    global_rows = index_ref[0] * warp_rows + local_rows
    valid = (global_rows >= 0) & (global_rows < part_count * warp_rows)

    def field(c):
        return jnp.concatenate([mid_ref[c], above_ref[c], below_ref[c]], axis=0)

    stiff = jnp.where(valid, field(ncomp), 1.0)
    root_stiff = jnp.sqrt(stiff)
    scale_term = couple_factor / root_stiff
    base_term = [field(c) / stiff for c in range(ncomp)]
    warp = [jnp.zeros((tall_rows, cols), jnp.float32) for c in range(ncomp)]
    for sweep_index in range(SWEEPS):
        for c in range(ncomp):
            spread = jnp.where(valid, root_stiff * warp[c], 0.0)
            beside_all = (
                pltpu.roll(spread, 1, 0)
                + pltpu.roll(spread, tall_rows - 1, 0)
                + pltpu.roll(spread, 1, 1)
                + pltpu.roll(spread, cols - 1, 1)
            )
            warp[c] = base_term[c] + scale_term * beside_all
    for c in range(ncomp):
        out_ref[c] = warp[c][:warp_rows]


def warp_sweeps(index, mid, above, below, part_count):
    ncomp = mid.shape[0] - 1
    return pl.pallas_call(
        functools.partial(warp_kernel, part_count),
        out_shape=jax.ShapeDtypeStruct((ncomp,) + mid.shape[1:], jnp.float32),
        in_specs=[pl.BlockSpec(memory_space=pltpu.SMEM)]
        + [pl.BlockSpec(memory_space=pltpu.VMEM)] * 3,
        out_specs=pl.BlockSpec(memory_space=pltpu.VMEM),
    )(index, mid, above, below)


def solution(mesh):
    placed = (
        P(None, "blk", "sub"),
        P(None, None, "blk", "sub"),
        P(None, "blk", "sub"),
        P(),
        P(),
        P(None, None, "blk", "sub"),
        P(("blk", "sub"), None),
    )
    return jax.shard_map(
        local,
        mesh=mesh,
        in_specs=placed,
        out_specs=(P(None, "blk", "sub"), P(None, ("blk", "sub"), None)),
        check_vma=False,
    )
```

```python
import functools
import numpy as np
import jax
import jax.numpy as jnp
from jax import lax
from jax.sharding import PartitionSpec as P
from jax.experimental import pallas as pl
from jax.experimental.pallas import tpu as pltpu

ITERS = 4
SWEEPS = 6


relax_factor = 0.8
couple_factor = 2.0 / 9.0
offsets_table = ((1, 0), (-1, 0), (2, 0), (-2, 0), (0, 1), (0, -1), (0, 2), (0, -2))
REACH = 2
LANES = 128


def ring_pairs(count, periodic):
    forward = [(i, i + 1) for i in range(count - 1)]
    if periodic:
        forward.append((count - 1, 0))
    backward = [(target, source) for source, target in forward]
    return forward, backward


TILE = 8
STRIPS = 16


def pack_kernel(adj_lo, adj_hi, jd_lo, jd_hi, fw_lo, fw_hi, below_lo, below_hi, above_lo, above_hi,
                low_ref, high_ref):
    strip = low_ref.shape[2] // STRIPS
    lanes = low_ref.shape[2]
    lane = lax.broadcasted_iota(jnp.int32, low_ref.shape[1:], 1)
    low = [jnp.zeros(low_ref.shape[1:], jnp.float32) for _ in range(low_ref.shape[0])]
    high = [jnp.zeros(high_ref.shape[1:], jnp.float32) for _ in range(high_ref.shape[0])]
    index = 0
    for lo_ref, hi_ref in ((adj_lo, adj_hi), (jd_lo, jd_hi), (fw_lo, fw_hi)):
        for f in range(lo_ref.shape[0]):
            group, slot = divmod(index, STRIPS)
            lo = jnp.concatenate([below_lo[index], lo_ref[f], above_lo[index]], axis=0)
            hi = jnp.concatenate([below_hi[index], hi_ref[f], above_hi[index]], axis=0)
            keep = (lane >= strip * slot) & (lane < strip * (slot + 1))
            low[group] = jnp.where(keep, pltpu.roll(lo, (strip * slot) % lanes, 1), low[group])
            high[group] = jnp.where(
                keep, pltpu.roll(hi, (strip * slot - (lanes - strip)) % lanes, 1), high[group]
            )
            index += 1
    for group in range(low_ref.shape[0]):
        low_ref[group] = low[group]
        high_ref[group] = high[group]


def pack_strips(fields, below, above, deep):
    rows_here, cols_here = fields[0].shape[1:]
    n_fields = below.shape[0]
    groups = -(-n_fields // STRIPS)
    last = cols_here // LANES - 1

    def chunk(x, c):
        return pl.BlockSpec((x.shape[0], x.shape[1], LANES), lambda i: (0, 0, c))

    specs = []
    args = []
    for x in list(fields) + [below, above]:
        specs += [chunk(x, 0), chunk(x, last)]
        args += [x, x]
    out = jax.ShapeDtypeStruct((groups, rows_here + 2 * deep, LANES), jnp.float32)
    return pl.pallas_call(
        pack_kernel,
        out_shape=(out, out),
        grid=(1,),
        in_specs=specs,
        out_specs=(pl.BlockSpec(out.shape, lambda i: (0, 0, 0)),) * 2,
    )(*args)


def flow_kernel(flux_ref, link_ref, adj_hbm, jd_hbm, fw_hbm, below_hbm, above_hbm, left_ref, right_ref,
                grad_ref, out_ref, sens_ref, tile_ref, buf0, buf1, sems):
    nf = out_ref.shape[0]
    rows_here = out_ref.shape[1]
    cols_here = out_ref.shape[2]
    width = tile_ref.shape[2]
    pad = 2 * TILE
    halo = below_hbm.shape[1]
    n_fields = tile_ref.shape[0]
    n_tiles = tile_ref.shape[1] // TILE
    jd0 = nf
    fw0 = nf + nf * nf
    copies = [
        pltpu.make_async_copy(adj_hbm, tile_ref.at[0:jd0, pad : pad + rows_here, 0:cols_here], sems.at[0]),
        pltpu.make_async_copy(jd_hbm, tile_ref.at[jd0:fw0, pad : pad + rows_here, 0:cols_here], sems.at[1]),
        pltpu.make_async_copy(fw_hbm, tile_ref.at[fw0:n_fields, pad : pad + rows_here, 0:cols_here], sems.at[2]),
        pltpu.make_async_copy(below_hbm, tile_ref.at[:, pad - halo : pad, 0:cols_here], sems.at[3]),
        pltpu.make_async_copy(
            above_hbm, tile_ref.at[:, pad + rows_here : pad + rows_here + halo, 0:cols_here], sems.at[4]
        ),
    ]
    for copy in copies:
        copy.start()
    for copy in copies:
        copy.wait()
    zeros = jnp.zeros((n_fields, pad - halo, width), jnp.float32)
    tile_ref[:, 0 : pad - halo, :] = zeros
    tile_ref[:, pad + rows_here + halo :, :] = zeros
    lanes = width - cols_here
    strip = lanes // STRIPS
    lane = lax.broadcasted_iota(jnp.int32, left_ref.shape[1:], 1)
    for index in range(n_fields):
        group, slot = divmod(index, STRIPS)
        after = pltpu.roll(right_ref[group], (-strip * slot) % lanes, 1)
        before = pltpu.roll(left_ref[group], (lanes - strip - strip * slot) % lanes, 1)
        edge = jnp.where(lane < halo, after, jnp.where(lane >= lanes - halo, before, 0.0))
        tile_ref[index, pad - halo : pad + rows_here + halo, cols_here:width] = edge
    link_above = link_ref[0]
    link_below = link_ref[1]
    bufs = (buf0, buf1)
    for iteration in range(ITERS):
        pin = tile_ref if iteration == 0 else bufs[(iteration - 1) % 2]
        pout = bufs[iteration % 2]
        last = iteration == ITERS - 1
        first = pad // TILE if last else 1
        stop = (pad + rows_here) // TILE if last else n_tiles - 1

        def body(t, carry, pin=pin, pout=pout):
            r0 = pl.multiple_of(t * TILE, TILE)
            win = [pin[g, pl.ds(r0 - TILE, 3 * TILE), :] for g in range(nf)]
            centre = [w[TILE : 2 * TILE] for w in win]
            rows = r0 - pad + lax.broadcasted_iota(jnp.int32, (TILE, width), 0)
            here = (rows + 2 * rows_here) // rows_here
            acc = []
            for f in range(nf):
                a = tile_ref[jd0 + f * nf, pl.ds(r0, TILE), :] * centre[0]
                for g in range(1, nf):
                    a = a + tile_ref[jd0 + f * nf + g, pl.ds(r0, TILE), :] * centre[g]
                acc.append(centre[f] + a)
            for direction in range(len(offsets_table)):
                row_step, col_step = offsets_table[direction]
                if row_step != 0:
                    shifted = [
                        pltpu.roll(w, (-row_step) % (3 * TILE), 0)[TILE : 2 * TILE] for w in win
                    ]
                    there = (rows + row_step + 2 * rows_here) // rows_here
                    link = jnp.where(jnp.minimum(here, there) < 2, link_below, link_above)
                    factor = jnp.where(here != there, link, 1.0)
                    shifted = [x * factor for x in shifted]
                else:
                    shifted = [pltpu.roll(c, (-col_step) % width, 1) for c in centre]
                weight = tile_ref[fw0 + direction, pl.ds(r0, TILE), :]
                for f in range(nf):
                    base = direction * nf * nf + f * nf
                    mixed = flux_ref[base] * shifted[0]
                    for g in range(1, nf):
                        mixed = mixed + flux_ref[base + g] * shifted[g]
                    acc[f] = acc[f] - weight * mixed
            for f in range(nf):
                src = tile_ref[f, pl.ds(r0, TILE), :]
                pout[f, pl.ds(r0, TILE), :] = centre[f] + relax_factor * (src - acc[f])
            return carry

        lax.fori_loop(first, stop, body, 0)
    final = bufs[(ITERS - 1) % 2]
    adjoint = [final[f, pad : pad + rows_here, 0:cols_here] for f in range(nf)]
    for f in range(nf):
        out_ref[f] = adjoint[f]
    for c in range(sens_ref.shape[0]):
        acc = grad_ref[c * nf].astype(jnp.float32) * adjoint[0]
        for f in range(1, nf):
            acc = acc + grad_ref[c * nf + f].astype(jnp.float32) * adjoint[f]
        sens_ref[c] = acc


def flow_iterations(flux_flat, links, adj, jd, fw, below, above, left, right, grad, width):
    nf, rows_here, cols_here = adj.shape
    n_fields = below.shape[0]
    tile_shape = (n_fields, rows_here + 4 * TILE, width)
    return pl.pallas_call(
        flow_kernel,
        out_shape=(
            jax.ShapeDtypeStruct((nf, rows_here, cols_here), jnp.float32),
            jax.ShapeDtypeStruct((grad.shape[0] // nf, rows_here, cols_here), jnp.float32),
        ),
        in_specs=[
            pl.BlockSpec(memory_space=pltpu.SMEM),
            pl.BlockSpec(memory_space=pltpu.SMEM),
        ]
        + [pl.BlockSpec(memory_space=pl.ANY)] * 5
        + [pl.BlockSpec(memory_space=pltpu.VMEM)] * 3,
        out_specs=(pl.BlockSpec(memory_space=pltpu.VMEM), pl.BlockSpec(memory_space=pltpu.VMEM)),
        scratch_shapes=[
            pltpu.VMEM(tile_shape, jnp.float32),
            pltpu.VMEM((nf,) + tile_shape[1:], jnp.float32),
            pltpu.VMEM((nf,) + tile_shape[1:], jnp.float32),
            pltpu.SemaphoreType.DMA((5,)),
        ],
        compiler_params=pltpu.CompilerParams(vmem_limit_bytes=48 * 1024 * 1024),
    )(flux_flat, links, adj, jd, fw, below, above, left, right, grad)


def local(adj_source, jac_diag, face_weights, flux_jac, face_link, node_grad, stiffness):
    block_index = lax.axis_index("blk")
    block_count = lax.axis_size("blk")
    link_above = face_link[block_index].astype(jnp.float32)
    link_below = face_link[(block_index + block_count - 1) % block_count].astype(jnp.float32)
    nf = adj_source.shape[0]
    rows_here = adj_source.shape[1]
    cols_here = adj_source.shape[2]
    deep = REACH * ITERS
    width = -(-(cols_here + 2 * deep) // LANES) * LANES

    fields = [adj_source, jac_diag.reshape((nf * nf,) + jac_diag.shape[2:]), face_weights]
    forward, backward = ring_pairs(block_count, True)
    from_below = lax.ppermute(
        jnp.concatenate([x[:, rows_here - deep :] for x in fields], axis=0), "blk", forward
    )
    from_above = lax.ppermute(jnp.concatenate([x[:, :deep] for x in fields], axis=0), "blk", backward)
    sub_count = lax.axis_size("sub")
    forward, backward = ring_pairs(sub_count, True)

    low_strips, high_strips = pack_strips(fields, from_below, from_above, deep)
    from_left = lax.ppermute(high_strips, "sub", forward)
    from_right = lax.ppermute(low_strips, "sub", backward)
    links = jnp.stack([link_above, link_below])
    adjoint, sensitivity = flow_iterations(
        flux_jac.reshape(-1), links, fields[0], fields[1], fields[2], from_below, from_above,
        from_left, from_right, node_grad.reshape((-1,) + node_grad.shape[2:]), width
    )

    moved = lax.all_to_all(sensitivity, "sub", split_axis=1, concat_axis=2, tiled=True)

    part_axis = ("blk", "sub")
    part_index = block_index * sub_count + lax.axis_index("sub")
    part_count = block_count * sub_count
    warp_rows = moved.shape[1]
    both = jnp.concatenate([moved, stiffness[None]], axis=0)
    forward, backward = ring_pairs(part_count, False)
    part_below = lax.ppermute(both, part_axis, forward)
    part_above = lax.ppermute(both, part_axis, backward)
    warp_adjoint = warp_sweeps(part_index.reshape(1), both, part_above, part_below, part_count)
    return (adjoint, warp_adjoint)


def warp_kernel(part_count, index_ref, mid_ref, above_ref, below_ref, out_ref):
    ncomp = out_ref.shape[0]
    warp_rows = out_ref.shape[1]
    cols = out_ref.shape[2]
    tall_rows = 3 * warp_rows
    rows = lax.broadcasted_iota(jnp.int32, (tall_rows, cols), 0)
    local_rows = jnp.where(rows < 2 * warp_rows, rows, rows - tall_rows)
    global_rows = index_ref[0] * warp_rows + local_rows
    valid = (global_rows >= 0) & (global_rows < part_count * warp_rows)

    def field(c):
        return jnp.concatenate([mid_ref[c], above_ref[c], below_ref[c]], axis=0)

    stiff = jnp.where(valid, field(ncomp), 1.0)
    root_stiff = jnp.sqrt(stiff)
    scale_term = couple_factor / root_stiff
    base_term = [field(c) / stiff for c in range(ncomp)]
    warp = [jnp.zeros((tall_rows, cols), jnp.float32) for c in range(ncomp)]
    for sweep_index in range(SWEEPS):
        for c in range(ncomp):
            spread = jnp.where(valid, root_stiff * warp[c], 0.0)
            beside_all = (
                pltpu.roll(spread, 1, 0)
                + pltpu.roll(spread, tall_rows - 1, 0)
                + pltpu.roll(spread, 1, 1)
                + pltpu.roll(spread, cols - 1, 1)
            )
            warp[c] = base_term[c] + scale_term * beside_all
    for c in range(ncomp):
        out_ref[c] = warp[c][:warp_rows]


def warp_sweeps(index, mid, above, below, part_count):
    ncomp = mid.shape[0] - 1
    return pl.pallas_call(
        functools.partial(warp_kernel, part_count),
        out_shape=jax.ShapeDtypeStruct((ncomp,) + mid.shape[1:], jnp.float32),
        in_specs=[pl.BlockSpec(memory_space=pltpu.SMEM)]
        + [pl.BlockSpec(memory_space=pltpu.VMEM)] * 3,
        out_specs=pl.BlockSpec(memory_space=pltpu.VMEM),
    )(index, mid, above, below)


def solution(mesh):
    placed = (
        P(None, "blk", "sub"),
        P(None, None, "blk", "sub"),
        P(None, "blk", "sub"),
        P(),
        P(),
        P(None, None, "blk", "sub"),
        P(("blk", "sub"), None),
    )
    return jax.shard_map(
        local,
        mesh=mesh,
        in_specs=placed,
        out_specs=(P(None, "blk", "sub"), P(None, ("blk", "sub"), None)),
        check_vma=False,
    )
```

```python
import functools
import numpy as np
import jax
import jax.numpy as jnp
from jax import lax
from jax.sharding import PartitionSpec as P
from jax.experimental import pallas as pl
from jax.experimental.pallas import tpu as pltpu

ITERS = 4
SWEEPS = 6


relax_factor = 0.8
couple_factor = 2.0 / 9.0
offsets_table = ((1, 0), (-1, 0), (2, 0), (-2, 0), (0, 1), (0, -1), (0, 2), (0, -2))
REACH = 2
LANES = 128


def ring_pairs(count, periodic):
    forward = [(i, i + 1) for i in range(count - 1)]
    if periodic:
        forward.append((count - 1, 0))
    backward = [(target, source) for source, target in forward]
    return forward, backward


TILE = 8
STRIPS = 16


def pack_kernel(adj_lo, adj_hi, jd_lo, jd_hi, fw_lo, fw_hi, below_lo, below_hi, above_lo, above_hi,
                low_ref, high_ref):
    strip = low_ref.shape[2] // STRIPS
    lanes = low_ref.shape[2]
    lane = lax.broadcasted_iota(jnp.int32, low_ref.shape[1:], 1)
    low = [jnp.zeros(low_ref.shape[1:], jnp.float32) for _ in range(low_ref.shape[0])]
    high = [jnp.zeros(high_ref.shape[1:], jnp.float32) for _ in range(high_ref.shape[0])]
    index = 0
    for lo_ref, hi_ref in ((adj_lo, adj_hi), (jd_lo, jd_hi), (fw_lo, fw_hi)):
        for f in range(lo_ref.shape[0]):
            group, slot = divmod(index, STRIPS)
            lo = jnp.concatenate([below_lo[index], lo_ref[f], above_lo[index]], axis=0)
            hi = jnp.concatenate([below_hi[index], hi_ref[f], above_hi[index]], axis=0)
            keep = (lane >= strip * slot) & (lane < strip * (slot + 1))
            low[group] = jnp.where(keep, pltpu.roll(lo, (strip * slot) % lanes, 1), low[group])
            high[group] = jnp.where(
                keep, pltpu.roll(hi, (strip * slot - (lanes - strip)) % lanes, 1), high[group]
            )
            index += 1
    for group in range(low_ref.shape[0]):
        low_ref[group] = low[group]
        high_ref[group] = high[group]


def pack_strips(fields, below, above, deep):
    rows_here, cols_here = fields[0].shape[1:]
    n_fields = below.shape[0]
    groups = -(-n_fields // STRIPS)
    last = cols_here // LANES - 1

    def chunk(x, c):
        return pl.BlockSpec((x.shape[0], x.shape[1], LANES), lambda i: (0, 0, c))

    specs = []
    args = []
    for x in list(fields) + [below, above]:
        specs += [chunk(x, 0), chunk(x, last)]
        args += [x, x]
    out = jax.ShapeDtypeStruct((groups, rows_here + 2 * deep, LANES), jnp.float32)
    return pl.pallas_call(
        pack_kernel,
        out_shape=(out, out),
        grid=(1,),
        in_specs=specs,
        out_specs=(pl.BlockSpec(out.shape, lambda i: (0, 0, 0)),) * 2,
    )(*args)


def flow_kernel(flux_ref, link_ref, adj_hbm, jd_hbm, fw_hbm, below_hbm, above_hbm, left_ref, right_ref,
                out_ref, tile_ref, buf0, buf1, sems):
    nf = out_ref.shape[0]
    rows_here = out_ref.shape[1]
    cols_here = out_ref.shape[2]
    width = tile_ref.shape[2]
    pad = 2 * TILE
    halo = below_hbm.shape[1]
    n_fields = tile_ref.shape[0]
    n_tiles = tile_ref.shape[1] // TILE
    jd0 = nf
    fw0 = nf + nf * nf
    copies = [
        pltpu.make_async_copy(adj_hbm, tile_ref.at[0:jd0, pad : pad + rows_here, 0:cols_here], sems.at[0]),
        pltpu.make_async_copy(jd_hbm, tile_ref.at[jd0:fw0, pad : pad + rows_here, 0:cols_here], sems.at[1]),
        pltpu.make_async_copy(fw_hbm, tile_ref.at[fw0:n_fields, pad : pad + rows_here, 0:cols_here], sems.at[2]),
        pltpu.make_async_copy(below_hbm, tile_ref.at[:, pad - halo : pad, 0:cols_here], sems.at[3]),
        pltpu.make_async_copy(
            above_hbm, tile_ref.at[:, pad + rows_here : pad + rows_here + halo, 0:cols_here], sems.at[4]
        ),
    ]
    for copy in copies:
        copy.start()
    for copy in copies:
        copy.wait()
    zeros = jnp.zeros((n_fields, pad - halo, width), jnp.float32)
    tile_ref[:, 0 : pad - halo, :] = zeros
    tile_ref[:, pad + rows_here + halo :, :] = zeros
    lanes = width - cols_here
    strip = lanes // STRIPS
    lane = lax.broadcasted_iota(jnp.int32, left_ref.shape[1:], 1)
    for index in range(n_fields):
        group, slot = divmod(index, STRIPS)
        after = pltpu.roll(right_ref[group], (-strip * slot) % lanes, 1)
        before = pltpu.roll(left_ref[group], (lanes - strip - strip * slot) % lanes, 1)
        edge = jnp.where(lane < halo, after, jnp.where(lane >= lanes - halo, before, 0.0))
        tile_ref[index, pad - halo : pad + rows_here + halo, cols_here:width] = edge
    link_above = link_ref[0]
    link_below = link_ref[1]
    bufs = (buf0, buf1)
    for iteration in range(ITERS):
        pin = tile_ref if iteration == 0 else bufs[(iteration - 1) % 2]
        pout = bufs[iteration % 2]
        last = iteration == ITERS - 1
        first = pad // TILE if last else 1
        stop = (pad + rows_here) // TILE if last else n_tiles - 1

        def body(t, carry, pin=pin, pout=pout):
            r0 = pl.multiple_of(t * TILE, TILE)
            centre = [pin[g, pl.ds(r0, TILE), :] for g in range(nf)]
            prev = [pin[g, pl.ds(r0 - TILE, TILE), :] for g in range(nf)]
            nxt = [pin[g, pl.ds(r0 + TILE, TILE), :] for g in range(nf)]
            sub = lax.broadcasted_iota(jnp.int32, (TILE, width), 0)
            rows = r0 - pad + sub
            here = (rows + 2 * rows_here) // rows_here
            acc = []
            for f in range(nf):
                a = tile_ref[jd0 + f * nf, pl.ds(r0, TILE), :] * centre[0]
                for g in range(1, nf):
                    a = a + tile_ref[jd0 + f * nf + g, pl.ds(r0, TILE), :] * centre[g]
                acc.append(centre[f] + a)
            for direction in range(len(offsets_table)):
                row_step, col_step = offsets_table[direction]
                if row_step != 0:
                    turn = (-row_step) % TILE
                    if row_step > 0:
                        shifted = [
                            jnp.where(sub < TILE - row_step, pltpu.roll(c, turn, 0), pltpu.roll(n, turn, 0))
                            for c, n in zip(centre, nxt)
                        ]
                    else:
                        shifted = [
                            jnp.where(sub >= -row_step, pltpu.roll(c, turn, 0), pltpu.roll(b, turn, 0))
                            for c, b in zip(centre, prev)
                        ]
                    there = (rows + row_step + 2 * rows_here) // rows_here
                    link = jnp.where(jnp.minimum(here, there) < 2, link_below, link_above)
                    factor = jnp.where(here != there, link, 1.0)
                    shifted = [x * factor for x in shifted]
                else:
                    shifted = [pltpu.roll(c, (-col_step) % width, 1) for c in centre]
                weight = tile_ref[fw0 + direction, pl.ds(r0, TILE), :]
                for f in range(nf):
                    base = direction * nf * nf + f * nf
                    mixed = flux_ref[base] * shifted[0]
                    for g in range(1, nf):
                        mixed = mixed + flux_ref[base + g] * shifted[g]
                    acc[f] = acc[f] - weight * mixed
            for f in range(nf):
                src = tile_ref[f, pl.ds(r0, TILE), :]
                pout[f, pl.ds(r0, TILE), :] = centre[f] + relax_factor * (src - acc[f])
            return carry

        lax.fori_loop(first, stop, body, 0)
    final = bufs[(ITERS - 1) % 2]
    out_ref[...] = final[:, pad : pad + rows_here, 0:cols_here]


def flow_iterations(flux_flat, links, adj, jd, fw, below, above, left, right, width):
    nf, rows_here, cols_here = adj.shape
    n_fields = below.shape[0]
    tile_shape = (n_fields, rows_here + 4 * TILE, width)
    return pl.pallas_call(
        flow_kernel,
        out_shape=jax.ShapeDtypeStruct((nf, rows_here, cols_here), jnp.float32),
        in_specs=[
            pl.BlockSpec(memory_space=pltpu.SMEM),
            pl.BlockSpec(memory_space=pltpu.SMEM),
        ]
        + [pl.BlockSpec(memory_space=pl.ANY)] * 5
        + [pl.BlockSpec(memory_space=pltpu.VMEM)] * 2,
        out_specs=pl.BlockSpec(memory_space=pltpu.VMEM),
        scratch_shapes=[
            pltpu.VMEM(tile_shape, jnp.float32),
            pltpu.VMEM((nf,) + tile_shape[1:], jnp.float32),
            pltpu.VMEM((nf,) + tile_shape[1:], jnp.float32),
            pltpu.SemaphoreType.DMA((5,)),
        ],
        compiler_params=pltpu.CompilerParams(vmem_limit_bytes=48 * 1024 * 1024),
    )(flux_flat, links, adj, jd, fw, below, above, left, right)


def local(adj_source, jac_diag, face_weights, flux_jac, face_link, node_grad, stiffness):
    block_index = lax.axis_index("blk")
    block_count = lax.axis_size("blk")
    link_above = face_link[block_index].astype(jnp.float32)
    link_below = face_link[(block_index + block_count - 1) % block_count].astype(jnp.float32)
    nf = adj_source.shape[0]
    rows_here = adj_source.shape[1]
    cols_here = adj_source.shape[2]
    deep = REACH * ITERS
    width = -(-(cols_here + 2 * deep) // LANES) * LANES

    fields = [adj_source, jac_diag.reshape((nf * nf,) + jac_diag.shape[2:]), face_weights]
    forward, backward = ring_pairs(block_count, True)
    from_below = lax.ppermute(
        jnp.concatenate([x[:, rows_here - deep :] for x in fields], axis=0), "blk", forward
    )
    from_above = lax.ppermute(jnp.concatenate([x[:, :deep] for x in fields], axis=0), "blk", backward)
    sub_count = lax.axis_size("sub")
    forward, backward = ring_pairs(sub_count, True)

    low_strips, high_strips = pack_strips(fields, from_below, from_above, deep)
    from_left = lax.ppermute(high_strips, "sub", forward)
    from_right = lax.ppermute(low_strips, "sub", backward)
    links = jnp.stack([link_above, link_below])
    adjoint = flow_iterations(
        flux_jac.reshape(-1), links, fields[0], fields[1], fields[2], from_below, from_above,
        from_left, from_right, width
    )

    sensitivity = jnp.einsum(
        "cfij,fij->cij", node_grad.astype(jnp.float32), adjoint, precision=lax.Precision.HIGHEST
    )
    moved = lax.all_to_all(sensitivity, "sub", split_axis=1, concat_axis=2, tiled=True)

    part_axis = ("blk", "sub")
    part_index = block_index * sub_count + lax.axis_index("sub")
    part_count = block_count * sub_count
    warp_rows = moved.shape[1]
    both = jnp.concatenate([moved, stiffness[None]], axis=0)
    forward, backward = ring_pairs(part_count, False)
    part_below = lax.ppermute(both, part_axis, forward)
    part_above = lax.ppermute(both, part_axis, backward)
    warp_adjoint = warp_sweeps(part_index.reshape(1), both, part_above, part_below, part_count)
    return (adjoint, warp_adjoint)


def warp_kernel(part_count, index_ref, mid_ref, above_ref, below_ref, out_ref):
    ncomp = out_ref.shape[0]
    warp_rows = out_ref.shape[1]
    cols = out_ref.shape[2]
    tall_rows = 3 * warp_rows
    rows = lax.broadcasted_iota(jnp.int32, (tall_rows, cols), 0)
    local_rows = jnp.where(rows < 2 * warp_rows, rows, rows - tall_rows)
    global_rows = index_ref[0] * warp_rows + local_rows
    valid = (global_rows >= 0) & (global_rows < part_count * warp_rows)

    def field(c):
        return jnp.concatenate([mid_ref[c], above_ref[c], below_ref[c]], axis=0)

    stiff = jnp.where(valid, field(ncomp), 1.0)
    root_stiff = jnp.sqrt(stiff)
    scale_term = couple_factor / root_stiff
    base_term = [field(c) / stiff for c in range(ncomp)]
    warp = [jnp.zeros((tall_rows, cols), jnp.float32) for c in range(ncomp)]
    for sweep_index in range(SWEEPS):
        for c in range(ncomp):
            spread = jnp.where(valid, root_stiff * warp[c], 0.0)
            beside_all = (
                pltpu.roll(spread, 1, 0)
                + pltpu.roll(spread, tall_rows - 1, 0)
                + pltpu.roll(spread, 1, 1)
                + pltpu.roll(spread, cols - 1, 1)
            )
            warp[c] = base_term[c] + scale_term * beside_all
    for c in range(ncomp):
        out_ref[c] = warp[c][:warp_rows]


def warp_sweeps(index, mid, above, below, part_count):
    ncomp = mid.shape[0] - 1
    return pl.pallas_call(
        functools.partial(warp_kernel, part_count),
        out_shape=jax.ShapeDtypeStruct((ncomp,) + mid.shape[1:], jnp.float32),
        in_specs=[pl.BlockSpec(memory_space=pltpu.SMEM)]
        + [pl.BlockSpec(memory_space=pltpu.VMEM)] * 3,
        out_specs=pl.BlockSpec(memory_space=pltpu.VMEM),
    )(index, mid, above, below)


def solution(mesh):
    placed = (
        P(None, "blk", "sub"),
        P(None, None, "blk", "sub"),
        P(None, "blk", "sub"),
        P(),
        P(),
        P(None, None, "blk", "sub"),
        P(("blk", "sub"), None),
    )
    return jax.shard_map(
        local,
        mesh=mesh,
        in_specs=placed,
        out_specs=(P(None, "blk", "sub"), P(None, ("blk", "sub"), None)),
        check_vma=False,
    )
```

```python
import functools
import numpy as np
import jax
import jax.numpy as jnp
from jax import lax
from jax.sharding import PartitionSpec as P
from jax.experimental import pallas as pl
from jax.experimental.pallas import tpu as pltpu

ITERS = 4
SWEEPS = 6


relax_factor = 0.8
couple_factor = 2.0 / 9.0
offsets_table = ((1, 0), (-1, 0), (2, 0), (-2, 0), (0, 1), (0, -1), (0, 2), (0, -2))
REACH = 2
LANES = 128


def ring_pairs(count, periodic):
    forward = [(i, i + 1) for i in range(count - 1)]
    if periodic:
        forward.append((count - 1, 0))
    backward = [(target, source) for source, target in forward]
    return forward, backward


TILE = 8
STRIPS = 16


def pack_kernel(adj_lo, adj_hi, jd_lo, jd_hi, fw_lo, fw_hi, below_lo, below_hi, above_lo, above_hi,
                low_ref, high_ref):
    strip = low_ref.shape[2] // STRIPS
    lanes = low_ref.shape[2]
    lane = lax.broadcasted_iota(jnp.int32, low_ref.shape[1:], 1)
    low = [jnp.zeros(low_ref.shape[1:], jnp.float32) for _ in range(low_ref.shape[0])]
    high = [jnp.zeros(high_ref.shape[1:], jnp.float32) for _ in range(high_ref.shape[0])]
    index = 0
    for lo_ref, hi_ref in ((adj_lo, adj_hi), (jd_lo, jd_hi), (fw_lo, fw_hi)):
        for f in range(lo_ref.shape[0]):
            group, slot = divmod(index, STRIPS)
            lo = jnp.concatenate([below_lo[index], lo_ref[f], above_lo[index]], axis=0)
            hi = jnp.concatenate([below_hi[index], hi_ref[f], above_hi[index]], axis=0)
            keep = (lane >= strip * slot) & (lane < strip * (slot + 1))
            low[group] = jnp.where(keep, pltpu.roll(lo, (strip * slot) % lanes, 1), low[group])
            high[group] = jnp.where(
                keep, pltpu.roll(hi, (strip * slot - (lanes - strip)) % lanes, 1), high[group]
            )
            index += 1
    for group in range(low_ref.shape[0]):
        low_ref[group] = low[group]
        high_ref[group] = high[group]


def pack_strips(fields, below, above, deep):
    rows_here, cols_here = fields[0].shape[1:]
    n_fields = below.shape[0]
    groups = -(-n_fields // STRIPS)
    last = cols_here // LANES - 1

    def chunk(x, c):
        return pl.BlockSpec((x.shape[0], x.shape[1], LANES), lambda i: (0, 0, c))

    specs = []
    args = []
    for x in list(fields) + [below, above]:
        specs += [chunk(x, 0), chunk(x, last)]
        args += [x, x]
    out = jax.ShapeDtypeStruct((groups, rows_here + 2 * deep, LANES), jnp.float32)
    return pl.pallas_call(
        pack_kernel,
        out_shape=(out, out),
        grid=(1,),
        in_specs=specs,
        out_specs=(pl.BlockSpec(out.shape, lambda i: (0, 0, 0)),) * 2,
    )(*args)


def flow_kernel(flux_ref, link_ref, adj_hbm, jd_hbm, fw_hbm, below_hbm, above_hbm, left_ref, right_ref,
                out_ref, tile_ref, buf0, buf1, sems):
    nf = out_ref.shape[0]
    rows_here = out_ref.shape[1]
    cols_here = out_ref.shape[2]
    width = tile_ref.shape[2]
    pad = 2 * TILE
    halo = below_hbm.shape[1]
    n_fields = tile_ref.shape[0]
    n_tiles = tile_ref.shape[1] // TILE
    jd0 = nf
    fw0 = nf + nf * nf
    copies = [
        pltpu.make_async_copy(adj_hbm, tile_ref.at[0:jd0, pad : pad + rows_here, 0:cols_here], sems.at[0]),
        pltpu.make_async_copy(jd_hbm, tile_ref.at[jd0:fw0, pad : pad + rows_here, 0:cols_here], sems.at[1]),
        pltpu.make_async_copy(fw_hbm, tile_ref.at[fw0:n_fields, pad : pad + rows_here, 0:cols_here], sems.at[2]),
        pltpu.make_async_copy(below_hbm, tile_ref.at[:, pad - halo : pad, 0:cols_here], sems.at[3]),
        pltpu.make_async_copy(
            above_hbm, tile_ref.at[:, pad + rows_here : pad + rows_here + halo, 0:cols_here], sems.at[4]
        ),
    ]
    for copy in copies:
        copy.start()
    for copy in copies:
        copy.wait()
    zeros = jnp.zeros((n_fields, pad - halo, width), jnp.float32)
    tile_ref[:, 0 : pad - halo, :] = zeros
    tile_ref[:, pad + rows_here + halo :, :] = zeros
    lanes = width - cols_here
    strip = lanes // STRIPS
    lane = lax.broadcasted_iota(jnp.int32, left_ref.shape[1:], 1)
    for index in range(n_fields):
        group, slot = divmod(index, STRIPS)
        after = pltpu.roll(right_ref[group], (-strip * slot) % lanes, 1)
        before = pltpu.roll(left_ref[group], (lanes - strip - strip * slot) % lanes, 1)
        edge = jnp.where(lane < halo, after, jnp.where(lane >= lanes - halo, before, 0.0))
        tile_ref[index, pad - halo : pad + rows_here + halo, cols_here:width] = edge
    link_above = link_ref[0]
    link_below = link_ref[1]
    bufs = (buf0, buf1)
    for iteration in range(ITERS):
        pin = tile_ref if iteration == 0 else bufs[(iteration - 1) % 2]
        pout = bufs[iteration % 2]
        last = iteration == ITERS - 1
        first = pad // TILE if last else 1
        stop = (pad + rows_here) // TILE if last else n_tiles - 1

        def body(t, carry, pin=pin, pout=pout):
            r0 = pl.multiple_of(t * TILE, TILE)
            centre = [pin[g, pl.ds(r0, TILE), :] for g in range(nf)]
            prev = [pin[g, pl.ds(r0 - TILE, TILE), :] for g in range(nf)]
            nxt = [pin[g, pl.ds(r0 + TILE, TILE), :] for g in range(nf)]
            sub = lax.broadcasted_iota(jnp.int32, (TILE, width), 0)
            rows = r0 - pad + sub
            here = (rows + 2 * rows_here) // rows_here
            acc = []
            for f in range(nf):
                a = tile_ref[jd0 + f * nf, pl.ds(r0, TILE), :] * centre[0]
                for g in range(1, nf):
                    a = a + tile_ref[jd0 + f * nf + g, pl.ds(r0, TILE), :] * centre[g]
                acc.append(centre[f] + a)
            for direction in range(len(offsets_table)):
                row_step, col_step = offsets_table[direction]
                if row_step != 0:
                    turn = (-row_step) % TILE
                    if row_step > 0:
                        shifted = [
                            jnp.where(sub < TILE - row_step, pltpu.roll(c, turn, 0), pltpu.roll(n, turn, 0))
                            for c, n in zip(centre, nxt)
                        ]
                    else:
                        shifted = [
                            jnp.where(sub >= -row_step, pltpu.roll(c, turn, 0), pltpu.roll(b, turn, 0))
                            for c, b in zip(centre, prev)
                        ]
                    there = (rows + row_step + 2 * rows_here) // rows_here
                    link = jnp.where(jnp.minimum(here, there) < 2, link_below, link_above)
                    factor = jnp.where(here != there, link, 1.0)
                else:
                    shifted = [pltpu.roll(c, (-col_step) % width, 1) for c in centre]
                weight = tile_ref[fw0 + direction, pl.ds(r0, TILE), :]
                if row_step != 0:
                    weight = weight * factor
                for f in range(nf):
                    base = direction * nf * nf + f * nf
                    mixed = flux_ref[base] * shifted[0]
                    for g in range(1, nf):
                        mixed = mixed + flux_ref[base + g] * shifted[g]
                    acc[f] = acc[f] - weight * mixed
            for f in range(nf):
                src = tile_ref[f, pl.ds(r0, TILE), :]
                pout[f, pl.ds(r0, TILE), :] = centre[f] + relax_factor * (src - acc[f])
            return carry

        lax.fori_loop(first, stop, body, 0)
    final = bufs[(ITERS - 1) % 2]
    out_ref[...] = final[:, pad : pad + rows_here, 0:cols_here]


def flow_iterations(flux_flat, links, adj, jd, fw, below, above, left, right, width):
    nf, rows_here, cols_here = adj.shape
    n_fields = below.shape[0]
    tile_shape = (n_fields, rows_here + 4 * TILE, width)
    return pl.pallas_call(
        flow_kernel,
        out_shape=jax.ShapeDtypeStruct((nf, rows_here, cols_here), jnp.float32),
        in_specs=[
            pl.BlockSpec(memory_space=pltpu.SMEM),
            pl.BlockSpec(memory_space=pltpu.SMEM),
        ]
        + [pl.BlockSpec(memory_space=pl.ANY)] * 5
        + [pl.BlockSpec(memory_space=pltpu.VMEM)] * 2,
        out_specs=pl.BlockSpec(memory_space=pltpu.VMEM),
        scratch_shapes=[
            pltpu.VMEM(tile_shape, jnp.float32),
            pltpu.VMEM((nf,) + tile_shape[1:], jnp.float32),
            pltpu.VMEM((nf,) + tile_shape[1:], jnp.float32),
            pltpu.SemaphoreType.DMA((5,)),
        ],
        compiler_params=pltpu.CompilerParams(vmem_limit_bytes=48 * 1024 * 1024),
    )(flux_flat, links, adj, jd, fw, below, above, left, right)


def local(adj_source, jac_diag, face_weights, flux_jac, face_link, node_grad, stiffness):
    block_index = lax.axis_index("blk")
    block_count = lax.axis_size("blk")
    link_above = face_link[block_index].astype(jnp.float32)
    link_below = face_link[(block_index + block_count - 1) % block_count].astype(jnp.float32)
    nf = adj_source.shape[0]
    rows_here = adj_source.shape[1]
    cols_here = adj_source.shape[2]
    deep = REACH * ITERS
    width = -(-(cols_here + 2 * deep) // LANES) * LANES

    fields = [adj_source, jac_diag.reshape((nf * nf,) + jac_diag.shape[2:]), face_weights]
    forward, backward = ring_pairs(block_count, True)
    from_below = lax.ppermute(
        jnp.concatenate([x[:, rows_here - deep :] for x in fields], axis=0), "blk", forward
    )
    from_above = lax.ppermute(jnp.concatenate([x[:, :deep] for x in fields], axis=0), "blk", backward)
    sub_count = lax.axis_size("sub")
    forward, backward = ring_pairs(sub_count, True)

    low_strips, high_strips = pack_strips(fields, from_below, from_above, deep)
    from_left = lax.ppermute(high_strips, "sub", forward)
    from_right = lax.ppermute(low_strips, "sub", backward)
    links = jnp.stack([link_above, link_below])
    adjoint = flow_iterations(
        flux_jac.reshape(-1), links, fields[0], fields[1], fields[2], from_below, from_above,
        from_left, from_right, width
    )

    sensitivity = jnp.einsum(
        "cfij,fij->cij", node_grad.astype(jnp.float32), adjoint, precision=lax.Precision.HIGHEST
    )
    moved = lax.all_to_all(sensitivity, "sub", split_axis=1, concat_axis=2, tiled=True)

    part_axis = ("blk", "sub")
    part_index = block_index * sub_count + lax.axis_index("sub")
    part_count = block_count * sub_count
    warp_rows = moved.shape[1]
    both = jnp.concatenate([moved, stiffness[None]], axis=0)
    forward, backward = ring_pairs(part_count, False)
    part_below = lax.ppermute(both, part_axis, forward)
    part_above = lax.ppermute(both, part_axis, backward)
    warp_adjoint = warp_sweeps(part_index.reshape(1), both, part_above, part_below, part_count)
    return (adjoint, warp_adjoint)


def warp_kernel(part_count, index_ref, mid_ref, above_ref, below_ref, out_ref):
    ncomp = out_ref.shape[0]
    warp_rows = out_ref.shape[1]
    cols = out_ref.shape[2]
    tall_rows = 3 * warp_rows
    rows = lax.broadcasted_iota(jnp.int32, (tall_rows, cols), 0)
    local_rows = jnp.where(rows < 2 * warp_rows, rows, rows - tall_rows)
    global_rows = index_ref[0] * warp_rows + local_rows
    valid = (global_rows >= 0) & (global_rows < part_count * warp_rows)

    def field(c):
        return jnp.concatenate([mid_ref[c], above_ref[c], below_ref[c]], axis=0)

    stiff = jnp.where(valid, field(ncomp), 1.0)
    root_stiff = jnp.sqrt(stiff)
    scale_term = couple_factor / root_stiff
    base_term = [field(c) / stiff for c in range(ncomp)]
    warp = list(base_term)
    for sweep_index in range(1, SWEEPS):
        for c in range(ncomp):
            spread = jnp.where(valid, root_stiff * warp[c], 0.0)
            beside_all = (
                pltpu.roll(spread, 1, 0)
                + pltpu.roll(spread, tall_rows - 1, 0)
                + pltpu.roll(spread, 1, 1)
                + pltpu.roll(spread, cols - 1, 1)
            )
            warp[c] = base_term[c] + scale_term * beside_all
    for c in range(ncomp):
        out_ref[c] = warp[c][:warp_rows]


def warp_sweeps(index, mid, above, below, part_count):
    ncomp = mid.shape[0] - 1
    return pl.pallas_call(
        functools.partial(warp_kernel, part_count),
        out_shape=jax.ShapeDtypeStruct((ncomp,) + mid.shape[1:], jnp.float32),
        in_specs=[pl.BlockSpec(memory_space=pltpu.SMEM)]
        + [pl.BlockSpec(memory_space=pltpu.VMEM)] * 3,
        out_specs=pl.BlockSpec(memory_space=pltpu.VMEM),
    )(index, mid, above, below)


def solution(mesh):
    placed = (
        P(None, "blk", "sub"),
        P(None, None, "blk", "sub"),
        P(None, "blk", "sub"),
        P(),
        P(),
        P(None, None, "blk", "sub"),
        P(("blk", "sub"), None),
    )
    return jax.shard_map(
        local,
        mesh=mesh,
        in_specs=placed,
        out_specs=(P(None, "blk", "sub"), P(None, ("blk", "sub"), None)),
        check_vma=False,
    )
```

```python
import functools
import numpy as np
import jax
import jax.numpy as jnp
from jax import lax
from jax.sharding import PartitionSpec as P
from jax.experimental import pallas as pl
from jax.experimental.pallas import tpu as pltpu

ITERS = 4
SWEEPS = 6


relax_factor = 0.8
couple_factor = 2.0 / 9.0
offsets_table = ((1, 0), (-1, 0), (2, 0), (-2, 0), (0, 1), (0, -1), (0, 2), (0, -2))
REACH = 2
LANES = 128


def ring_pairs(count, periodic):
    forward = [(i, i + 1) for i in range(count - 1)]
    if periodic:
        forward.append((count - 1, 0))
    backward = [(target, source) for source, target in forward]
    return forward, backward


TILE = 8
STRIPS = 16


def pack_kernel(adj_lo, adj_hi, jd_lo, jd_hi, fw_lo, fw_hi, below_lo, below_hi, above_lo, above_hi,
                low_ref, high_ref):
    strip = low_ref.shape[2] // STRIPS
    lanes = low_ref.shape[2]
    halo = below_lo.shape[1]
    middle = adj_lo.shape[1]
    pieces = ((0, halo), (halo, halo + middle), (halo + middle, 2 * halo + middle))
    groups = low_ref.shape[0]
    for part, (start, stop) in enumerate(pieces):
        lane = lax.broadcasted_iota(jnp.int32, (stop - start, lanes), 1)
        low = [jnp.zeros((stop - start, lanes), jnp.float32) for _ in range(groups)]
        high = [jnp.zeros((stop - start, lanes), jnp.float32) for _ in range(groups)]
        index = 0
        for lo_ref, hi_ref in ((adj_lo, adj_hi), (jd_lo, jd_hi), (fw_lo, fw_hi)):
            for f in range(lo_ref.shape[0]):
                group, slot = divmod(index, STRIPS)
                if part == 0:
                    lo, hi = below_lo[index], below_hi[index]
                elif part == 1:
                    lo, hi = lo_ref[f], hi_ref[f]
                else:
                    lo, hi = above_lo[index], above_hi[index]
                keep = (lane >= strip * slot) & (lane < strip * (slot + 1))
                low[group] = jnp.where(keep, pltpu.roll(lo, (strip * slot) % lanes, 1), low[group])
                high[group] = jnp.where(
                    keep, pltpu.roll(hi, (strip * slot - (lanes - strip)) % lanes, 1), high[group]
                )
                index += 1
        for group in range(groups):
            low_ref[group, start:stop] = low[group]
            high_ref[group, start:stop] = high[group]


def pack_strips(fields, below, above, deep):
    rows_here, cols_here = fields[0].shape[1:]
    n_fields = below.shape[0]
    groups = -(-n_fields // STRIPS)
    last = cols_here // LANES - 1

    def chunk(x, c):
        return pl.BlockSpec((x.shape[0], x.shape[1], LANES), lambda i: (0, 0, c))

    specs = []
    args = []
    for x in list(fields) + [below, above]:
        specs += [chunk(x, 0), chunk(x, last)]
        args += [x, x]
    out = jax.ShapeDtypeStruct((groups, rows_here + 2 * deep, LANES), jnp.float32)
    return pl.pallas_call(
        pack_kernel,
        out_shape=(out, out),
        grid=(1,),
        in_specs=specs,
        out_specs=(pl.BlockSpec(out.shape, lambda i: (0, 0, 0)),) * 2,
    )(*args)


def flow_kernel(flux_ref, link_ref, adj_hbm, jd_hbm, fw_hbm, below_hbm, above_hbm, left_ref, right_ref,
                out_ref, tile_ref, buf0, buf1, sems):
    nf = out_ref.shape[0]
    rows_here = out_ref.shape[1]
    cols_here = out_ref.shape[2]
    width = tile_ref.shape[2]
    pad = 2 * TILE
    halo = below_hbm.shape[1]
    n_fields = tile_ref.shape[0]
    n_tiles = tile_ref.shape[1] // TILE
    jd0 = nf
    fw0 = nf + nf * nf
    copies = [
        pltpu.make_async_copy(adj_hbm, tile_ref.at[0:jd0, pad : pad + rows_here, 0:cols_here], sems.at[0]),
        pltpu.make_async_copy(jd_hbm, tile_ref.at[jd0:fw0, pad : pad + rows_here, 0:cols_here], sems.at[1]),
        pltpu.make_async_copy(fw_hbm, tile_ref.at[fw0:n_fields, pad : pad + rows_here, 0:cols_here], sems.at[2]),
        pltpu.make_async_copy(below_hbm, tile_ref.at[:, pad - halo : pad, 0:cols_here], sems.at[3]),
        pltpu.make_async_copy(
            above_hbm, tile_ref.at[:, pad + rows_here : pad + rows_here + halo, 0:cols_here], sems.at[4]
        ),
    ]
    for copy in copies:
        copy.start()
    for copy in copies:
        copy.wait()
    zeros = jnp.zeros((n_fields, pad - halo, width), jnp.float32)
    tile_ref[:, 0 : pad - halo, :] = zeros
    tile_ref[:, pad + rows_here + halo :, :] = zeros
    lanes = width - cols_here
    strip = lanes // STRIPS
    lane = lax.broadcasted_iota(jnp.int32, left_ref.shape[1:], 1)
    for index in range(n_fields):
        group, slot = divmod(index, STRIPS)
        after = pltpu.roll(right_ref[group], (-strip * slot) % lanes, 1)
        before = pltpu.roll(left_ref[group], (lanes - strip - strip * slot) % lanes, 1)
        edge = jnp.where(lane < halo, after, jnp.where(lane >= lanes - halo, before, 0.0))
        tile_ref[index, pad - halo : pad + rows_here + halo, cols_here:width] = edge
    link_above = link_ref[0]
    link_below = link_ref[1]
    bufs = (buf0, buf1)
    for iteration in range(ITERS):
        pin = tile_ref if iteration == 0 else bufs[(iteration - 1) % 2]
        pout = bufs[iteration % 2]
        last = iteration == ITERS - 1
        first = pad // TILE if last else 1
        stop = (pad + rows_here) // TILE if last else n_tiles - 1

        def body(t, carry, pin=pin, pout=pout):
            r0 = pl.multiple_of(t * TILE, TILE)
            centre = [pin[g, pl.ds(r0, TILE), :] for g in range(nf)]
            prev = [pin[g, pl.ds(r0 - TILE, TILE), :] for g in range(nf)]
            nxt = [pin[g, pl.ds(r0 + TILE, TILE), :] for g in range(nf)]
            sub = lax.broadcasted_iota(jnp.int32, (TILE, width), 0)
            rows = r0 - pad + sub
            here = (rows + 2 * rows_here) // rows_here
            acc = []
            for f in range(nf):
                a = tile_ref[jd0 + f * nf, pl.ds(r0, TILE), :] * centre[0]
                for g in range(1, nf):
                    a = a + tile_ref[jd0 + f * nf + g, pl.ds(r0, TILE), :] * centre[g]
                acc.append(centre[f] + a)
            for direction in range(len(offsets_table)):
                row_step, col_step = offsets_table[direction]
                if row_step != 0:
                    turn = (-row_step) % TILE
                    if row_step > 0:
                        shifted = [
                            jnp.where(sub < TILE - row_step, pltpu.roll(c, turn, 0), pltpu.roll(n, turn, 0))
                            for c, n in zip(centre, nxt)
                        ]
                    else:
                        shifted = [
                            jnp.where(sub >= -row_step, pltpu.roll(c, turn, 0), pltpu.roll(b, turn, 0))
                            for c, b in zip(centre, prev)
                        ]
                    there = (rows + row_step + 2 * rows_here) // rows_here
                    link = jnp.where(jnp.minimum(here, there) < 2, link_below, link_above)
                    factor = jnp.where(here != there, link, 1.0)
                else:
                    shifted = [pltpu.roll(c, (-col_step) % width, 1) for c in centre]
                weight = tile_ref[fw0 + direction, pl.ds(r0, TILE), :]
                if row_step != 0:
                    weight = weight * factor
                for f in range(nf):
                    base = direction * nf * nf + f * nf
                    mixed = flux_ref[base] * shifted[0]
                    for g in range(1, nf):
                        mixed = mixed + flux_ref[base + g] * shifted[g]
                    acc[f] = acc[f] - weight * mixed
            for f in range(nf):
                src = tile_ref[f, pl.ds(r0, TILE), :]
                pout[f, pl.ds(r0, TILE), :] = centre[f] + relax_factor * (src - acc[f])
            return carry

        lax.fori_loop(first, stop, body, 0)
    final = bufs[(ITERS - 1) % 2]
    out_ref[...] = final[:, pad : pad + rows_here, 0:cols_here]


def flow_iterations(flux_flat, links, adj, jd, fw, below, above, left, right, width):
    nf, rows_here, cols_here = adj.shape
    n_fields = below.shape[0]
    tile_shape = (n_fields, rows_here + 4 * TILE, width)
    return pl.pallas_call(
        flow_kernel,
        out_shape=jax.ShapeDtypeStruct((nf, rows_here, cols_here), jnp.float32),
        in_specs=[
            pl.BlockSpec(memory_space=pltpu.SMEM),
            pl.BlockSpec(memory_space=pltpu.SMEM),
        ]
        + [pl.BlockSpec(memory_space=pl.ANY)] * 5
        + [pl.BlockSpec(memory_space=pltpu.VMEM)] * 2,
        out_specs=pl.BlockSpec(memory_space=pltpu.VMEM),
        scratch_shapes=[
            pltpu.VMEM(tile_shape, jnp.float32),
            pltpu.VMEM((nf,) + tile_shape[1:], jnp.float32),
            pltpu.VMEM((nf,) + tile_shape[1:], jnp.float32),
            pltpu.SemaphoreType.DMA((5,)),
        ],
        compiler_params=pltpu.CompilerParams(vmem_limit_bytes=48 * 1024 * 1024),
    )(flux_flat, links, adj, jd, fw, below, above, left, right)


def local(adj_source, jac_diag, face_weights, flux_jac, face_link, node_grad, stiffness):
    block_index = lax.axis_index("blk")
    block_count = lax.axis_size("blk")
    link_above = face_link[block_index].astype(jnp.float32)
    link_below = face_link[(block_index + block_count - 1) % block_count].astype(jnp.float32)
    nf = adj_source.shape[0]
    rows_here = adj_source.shape[1]
    cols_here = adj_source.shape[2]
    deep = REACH * ITERS
    width = -(-(cols_here + 2 * deep) // LANES) * LANES

    fields = [adj_source, jac_diag.reshape((nf * nf,) + jac_diag.shape[2:]), face_weights]
    forward, backward = ring_pairs(block_count, True)
    from_below = lax.ppermute(
        jnp.concatenate([x[:, rows_here - deep :] for x in fields], axis=0), "blk", forward
    )
    from_above = lax.ppermute(jnp.concatenate([x[:, :deep] for x in fields], axis=0), "blk", backward)
    sub_count = lax.axis_size("sub")
    forward, backward = ring_pairs(sub_count, True)

    low_strips, high_strips = pack_strips(fields, from_below, from_above, deep)
    from_left = lax.ppermute(high_strips, "sub", forward)
    from_right = lax.ppermute(low_strips, "sub", backward)
    links = jnp.stack([link_above, link_below])
    adjoint = flow_iterations(
        flux_jac.reshape(-1), links, fields[0], fields[1], fields[2], from_below, from_above,
        from_left, from_right, width
    )

    sensitivity = jnp.einsum(
        "cfij,fij->cij", node_grad.astype(jnp.float32), adjoint, precision=lax.Precision.HIGHEST
    )
    moved = lax.all_to_all(sensitivity, "sub", split_axis=1, concat_axis=2, tiled=True)

    part_axis = ("blk", "sub")
    part_index = block_index * sub_count + lax.axis_index("sub")
    part_count = block_count * sub_count
    warp_rows = moved.shape[1]
    both = jnp.concatenate([moved, stiffness[None]], axis=0)
    forward, backward = ring_pairs(part_count, False)
    part_below = lax.ppermute(both, part_axis, forward)
    part_above = lax.ppermute(both, part_axis, backward)
    warp_adjoint = warp_sweeps(part_index.reshape(1), both, part_above, part_below, part_count)
    return (adjoint, warp_adjoint)


def warp_kernel(part_count, index_ref, mid_ref, above_ref, below_ref, out_ref):
    ncomp = out_ref.shape[0]
    warp_rows = out_ref.shape[1]
    cols = out_ref.shape[2]
    tall_rows = 3 * warp_rows
    rows = lax.broadcasted_iota(jnp.int32, (tall_rows, cols), 0)
    local_rows = jnp.where(rows < 2 * warp_rows, rows, rows - tall_rows)
    global_rows = index_ref[0] * warp_rows + local_rows
    valid = (global_rows >= 0) & (global_rows < part_count * warp_rows)

    def field(c):
        return jnp.concatenate([mid_ref[c], above_ref[c], below_ref[c]], axis=0)

    stiff = jnp.where(valid, field(ncomp), 1.0)
    root_stiff = jnp.sqrt(stiff)
    scale_term = couple_factor / root_stiff
    base_term = [field(c) / stiff for c in range(ncomp)]
    warp = list(base_term)
    for sweep_index in range(1, SWEEPS):
        for c in range(ncomp):
            spread = jnp.where(valid, root_stiff * warp[c], 0.0)
            beside_all = (
                pltpu.roll(spread, 1, 0)
                + pltpu.roll(spread, tall_rows - 1, 0)
                + pltpu.roll(spread, 1, 1)
                + pltpu.roll(spread, cols - 1, 1)
            )
            warp[c] = base_term[c] + scale_term * beside_all
    for c in range(ncomp):
        out_ref[c] = warp[c][:warp_rows]


def warp_sweeps(index, mid, above, below, part_count):
    ncomp = mid.shape[0] - 1
    return pl.pallas_call(
        functools.partial(warp_kernel, part_count),
        out_shape=jax.ShapeDtypeStruct((ncomp,) + mid.shape[1:], jnp.float32),
        in_specs=[pl.BlockSpec(memory_space=pltpu.SMEM)]
        + [pl.BlockSpec(memory_space=pltpu.VMEM)] * 3,
        out_specs=pl.BlockSpec(memory_space=pltpu.VMEM),
    )(index, mid, above, below)


def solution(mesh):
    placed = (
        P(None, "blk", "sub"),
        P(None, None, "blk", "sub"),
        P(None, "blk", "sub"),
        P(),
        P(),
        P(None, None, "blk", "sub"),
        P(("blk", "sub"), None),
    )
    return jax.shard_map(
        local,
        mesh=mesh,
        in_specs=placed,
        out_specs=(P(None, "blk", "sub"), P(None, ("blk", "sub"), None)),
        check_vma=False,
    )
```
